128 devices in a mesh: seq: 16 (over z, x), heads: 8 (over y, core).
Axes of the slice: x: 4, y: 4, z: 4, core: 2. Of those that a mesh axis runs over, the one named last changes fastest.
Arguments:
- audio: bfloat16 [4096, 1280], P('seq'), may hold values from -6 to 6
- ln_gain: float32 [1280], replicated, may hold values from 0.25 to 1.75
- ln_shift: float32 [1280], replicated, may hold values from -3 to 3
- enc_wq: bfloat16 [1280, 1024], P(None, 'heads'), may hold values from -0.15625 to 0.15625
- enc_bq: float32 [1024], P('heads'), may hold values from -3 to 3
- enc_wk: bfloat16 [1280, 1024], P(None, 'heads'), may hold values from -4 to 4
- enc_wv: bfloat16 [1280, 1024], P(None, 'heads'), may hold values from -0.15625 to 0.15625
- enc_bv: float32 [1024], P('heads'), may hold values from -3 to 3
- enc_wo: bfloat16 [1024, 1280], P('heads'), may hold values from -0.1875 to 0.1875
- enc_bo: float32 [1280], replicated, may hold values from -3 to 3
- windows: int32 [16], P('heads'), may hold values from 1 to 128, as said below
- dec_wkv: bfloat16 [1280, 8, 256], replicated, may hold values from -4 to 4
- dec_bv: float32 [8, 128], replicated, may hold values from -3 to 3
- text: bfloat16 [8192, 8192], P('seq'), may hold values from -6 to 6
- norm_gain: float32 [8192], replicated, may hold values from 0.25 to 1.75
- dec_wq: bfloat16 [8192, 4096], P('seq', 'heads'), may hold values from -0.0625 to 0.0625
- dec_bq: float32 [4096], P('heads'), may hold values from -3 to 3
- dec_wo: bfloat16 [4096, 8192], P('heads', 'seq'), may hold values from -0.125 to 0.125
- span_start: int32 [8192], P('seq'), may hold values from 0 to 3840, as said below
- span_len: int32 [8192], P('seq'), may hold values from 1 to 256, as said below
Outputs:
- enc_out: bfloat16 [4096, 1280], P(('seq', 'heads'))
- dec_out: bfloat16 [8192, 8192], P('seq', 'heads')
The draws below stay inside these ranges and needn't reach their ends.
Inputs may be any that keep to these rules, and one draw needn't show every extreme that they name: `windows`: every head's window is 1 to 128; some head has exactly 128 and some head exactly 1. `span_start`: row r's band begins between r * 256 // 512 - 255 and r * 256 // 512, and never before frame 0 or after 4096 - 256; row 0 begins at 0 and the last row at 3840; the last row of every aligned block of 512 rows but the final one begins exactly at r * 256 // 512. `span_len`: row 0 has 256 valid frames and row 1 has one; the last row of every aligned block of 512 rows has 256, unless it is row 1.
All inputs are finite; a program needn't handle non-finite values.
Results may differ from the reference program's by a relative error of at most 0.025.
Values may be sent and summed in bfloat16 or wider, within the bound.
No kernel may reach another device: no remote copies, remote signals or barrier semaphores. Data moves between devices by JAX's collectives and lax.ppermute only.
A program may use at most 128 MiB of HBM per device.

```python
import jax
import jax.numpy as jnp
from jax import lax

D_ENC = 1280
EH = 16
EHD = 64
EWIN = 128
FR_SEQ = 256
FRAMES = 4096
D = 8192
KVG = 8
QPG = 4
HD = 128
GL = 1
BAND = 256
ROWS_DEV = 512
ROWS = 8192
N_SEQ = 16
N_HEADS = 8


def draw_windows(key, part):
    key_one, key_two = jax.random.split(key)
    widths = jax.random.randint(key_one, (EH,), 1, EWIN + 1, dtype=jnp.int32)
    shuffled = jax.random.permutation(key_two, EH)
    return widths.at[shuffled[0]].set(EWIN).at[shuffled[1]].set(1)


def draw_span_start(key, part):
    row_ids = jnp.arange(ROWS, dtype=jnp.int32)
    centres = row_ids * FR_SEQ // ROWS_DEV
    offsets = jax.random.randint(key, (ROWS,), 0, BAND, dtype=jnp.int32)
    block_last = row_ids % ROWS_DEV == ROWS_DEV - 1
    offsets = jnp.where(block_last, jnp.zeros_like(offsets), offsets)
    begins = jnp.clip(centres - offsets, 0, FRAMES - BAND)
    return begins.at[ROWS - 1].set(FRAMES - BAND)


def draw_span_len(key, part):
    row_ids = jnp.arange(ROWS, dtype=jnp.int32)
    counts = jax.random.randint(key, (ROWS,), 1, BAND + 1, dtype=jnp.int32)
    block_last = row_ids % ROWS_DEV == ROWS_DEV - 1
    counts = jnp.where(block_last, jnp.full_like(counts, BAND), counts)
    return counts.at[0].set(BAND).at[1].set(1)


def shift_values(key):
    return 0.5 * jax.random.truncated_normal(jax.random.fold_in(key, 101), -6.0, 6.0, (D_ENC,), jnp.float32)


def output_bias_values(key):
    return 0.5 * jax.random.truncated_normal(jax.random.fold_in(key, 201), -6.0, 6.0, (D_ENC,), jnp.float32)


def draw_audio(key, part):
    values = jax.random.truncated_normal(jax.random.fold_in(key, 301), -6.0, 6.0, (FRAMES, D_ENC), jnp.float32)
    return values.astype(jnp.bfloat16)


def draw_ln_shift(key, part):
    return shift_values(key)


def draw_enc_bo(key, part):
    return output_bias_values(key)


def draw_enc_wk(key, part):
    column_count = EH * EHD
    base_draw = jax.random.truncated_normal(jax.random.fold_in(key, 102), -6.0, 6.0, (D_ENC, column_count), jnp.float32) * D_ENC ** (-0.5)
    return base_draw.astype(jnp.bfloat16)


def draw_dec_wkv(key, part):
    base_draw = jax.random.truncated_normal(jax.random.fold_in(key, 202), -6.0, 6.0, (D_ENC, KVG, 2 * HD), jnp.float32) * D_ENC ** (-0.5)
    return base_draw.astype(jnp.bfloat16)


def strengthened(result, own_key, source, target, blocks, factor):
    owner, partner = [(jnp.arange(result.shape[position]) // (result.shape[position] // blocks)).reshape([-1 if axis == position else 1 for axis in range(result.ndim)]) for position in (source, target)]
    chosen = jax.random.permutation(own_key, blocks)[partner]
    strong = (owner == chosen) | (owner == (partner + blocks // 2) % blocks)
    return jnp.where(strong, factor * result, result)


def block_scale(key, shape, pieces, least, top_value):
    factor_of, own = 1.0, jax.random.fold_in(key, 6)
    for position, parts in pieces:
        steps = jnp.exp(jax.random.uniform(jax.random.fold_in(own, position), (parts,), jnp.float32, least / len(pieces), top_value / len(pieces)))
        factor_of = factor_of * jnp.repeat(steps, shape[position] // parts).reshape([-1 if axis == position else 1 for axis in range(len(shape))])
    return factor_of


def normal_values(rng, dims, scale, bound, cuts=(), held_as=jnp.bfloat16):
    factor_of = block_scale(rng, dims, cuts, -0.22, 0.18) if cuts else 1.0
    result = jax.random.normal(rng, dims, jnp.float32) * scale * factor_of
    return jnp.minimum(jnp.maximum(result, -bound), bound).astype(held_as)


def heavy_noise(own_key, dims, deviation, limit, pieces, heavy, kind=jnp.bfloat16):
    result = deviation * jax.random.normal(own_key, dims, jnp.float32)
    if pieces:
        result = result * block_scale(own_key, dims, pieces, -0.22, 0.18)
    return jnp.clip(strengthened(result, jax.random.fold_in(own_key, 3), *heavy), -limit, limit).astype(kind)


def setup_inputs(seed: int = 0) -> dict:
    arg_keys = jax.random.split(jax.random.key(seed), 21)
    audio = draw_audio(jax.random.fold_in(arg_keys[20], 71), 0)
    ln_gain = jnp.clip(1.0 + 0.15 * jax.random.normal(arg_keys[1], (D_ENC,), jnp.float32), 0.25, 1.75)
    ln_shift = draw_ln_shift(jax.random.fold_in(arg_keys[20], 71), 0)
    enc_wq = normal_values(arg_keys[3], (D_ENC, EH * EHD), D_ENC ** -0.5, 0.15625, ((1, 8),))
    enc_bq = normal_values(arg_keys[4], (EH * EHD,), 0.5, 3.0, ((0, 8),), jnp.float32)
    enc_wk = draw_enc_wk(jax.random.fold_in(arg_keys[20], 71), 0)
    enc_wv = normal_values(arg_keys[6], (D_ENC, EH * EHD), D_ENC ** -0.5, 0.15625, ((1, 8),))
    enc_bv = normal_values(arg_keys[7], (EH * EHD,), 0.5, 3.0, ((0, 8),), jnp.float32)
    enc_wo = normal_values(arg_keys[8], (EH * EHD, D_ENC), (EH * EHD) ** -0.5, 0.1875, ((0, 8),))
    enc_bo = draw_enc_bo(jax.random.fold_in(arg_keys[20], 71), 0)
    windows = draw_windows(jax.random.fold_in(arg_keys[20], 71), 0)
    dec_wkv = draw_dec_wkv(jax.random.fold_in(arg_keys[20], 71), 0)
    dec_bv = normal_values(arg_keys[12], (KVG, HD), 0.5, 3.0, (), jnp.float32)
    text = normal_values(arg_keys[13], (ROWS, D), 1.0, 6.0, ((0, 16),))
    norm_gain = jnp.clip(1.0 + 0.15 * jax.random.normal(arg_keys[14], (D,), jnp.float32), 0.25, 1.75)
    dec_wq = normal_values(arg_keys[15], (D, KVG * QPG * HD), D ** -0.5, 0.0625, ((0, 16), (1, 8)))
    dec_bq = normal_values(arg_keys[16], (KVG * QPG * HD,), 0.5, 3.0, ((0, 8),), jnp.float32)
    dec_wo = heavy_noise(arg_keys[17], (KVG * QPG * HD, D), (KVG * QPG * HD) ** -0.5, 0.125, ((0, 8), (1, 16)), (0, 1, 16, 2.0))
    span_start = draw_span_start(jax.random.fold_in(arg_keys[20], 71), 0)
    span_len = draw_span_len(jax.random.fold_in(arg_keys[20], 71), 0)
    return dict(audio=audio, ln_gain=ln_gain, ln_shift=ln_shift, enc_wq=enc_wq, enc_bq=enc_bq, enc_wk=enc_wk, enc_wv=enc_wv, enc_bv=enc_bv, enc_wo=enc_wo, enc_bo=enc_bo, windows=windows, dec_wkv=dec_wkv, dec_bv=dec_bv, text=text, norm_gain=norm_gain, dec_wq=dec_wq, dec_bq=dec_bq, dec_wo=dec_wo, span_start=span_start, span_len=span_len)


def layer_norm(values, gain, shift):
    values = values.astype(jnp.float32)
    centre = values - lax.optimization_barrier(jnp.mean(values, axis=-1, keepdims=True))
    spread = lax.optimization_barrier(jnp.mean(centre * centre, axis=-1, keepdims=True))
    return centre * lax.rsqrt(spread + 1e-05) * gain + shift

def rms_norm(values, gain):
    values = values.astype(jnp.float32)
    return values * lax.rsqrt(lax.optimization_barrier(jnp.mean(values * values, axis=-1, keepdims=True)) + 1e-06) * gain

def masked_softmax(scores, valid):
    highest = lax.optimization_barrier(jnp.max(jnp.where(valid, scores, -jnp.inf), axis=-1, keepdims=True))
    raised = jnp.where(valid, jnp.exp(scores - highest), jnp.zeros_like(scores))
    return (raised / lax.optimization_barrier(jnp.sum(raised, axis=-1, keepdims=True))).astype(jnp.bfloat16)

def reference(audio, ln_gain, ln_shift, enc_wq, enc_bq, enc_wk, enc_wv, enc_bv, enc_wo, enc_bo, windows, dec_wkv, dec_bv, text, norm_gain, dec_wq, dec_bq, dec_wo, span_start, span_len):
    hidden = layer_norm(audio, ln_gain, ln_shift).astype(jnp.bfloat16)
    enc_query = (jnp.dot(hidden, enc_wq, preferred_element_type=jnp.float32) + enc_bq).astype(jnp.bfloat16)
    enc_keys = jnp.dot(hidden, enc_wk, preferred_element_type=jnp.float32).astype(jnp.bfloat16)
    enc_values = (jnp.dot(hidden, enc_wv, preferred_element_type=jnp.float32) + enc_bv).astype(jnp.bfloat16)
    enc_query = enc_query.reshape(FRAMES, EH, EHD)
    pad_keys = jnp.pad(enc_keys.reshape(FRAMES, EH, EHD), ((EWIN, EWIN), (0, 0), (0, 0)))
    pad_values = jnp.pad(enc_values.reshape(FRAMES, EH, EHD), ((EWIN, EWIN), (0, 0), (0, 0)))
    extent = FR_SEQ + 2 * EWIN

    def enc_block(block_index):
        first_frame = block_index * FR_SEQ
        query_block = lax.dynamic_slice_in_dim(enc_query, first_frame, FR_SEQ, 0).astype(jnp.float32)
        key_block = lax.dynamic_slice_in_dim(pad_keys, first_frame, extent, 0).astype(jnp.float32)
        value_block = lax.dynamic_slice_in_dim(pad_values, first_frame, extent, 0).astype(jnp.float32)
        scores = jnp.einsum('qhd,khd->hqk', query_block, key_block) * EHD ** (-0.5)
        row_frames = first_frame + jnp.arange(FR_SEQ, dtype=jnp.int32)
        col_frames = first_frame - EWIN + jnp.arange(extent, dtype=jnp.int32)
        distance = jnp.abs(row_frames[:, None] - col_frames[None, :])
        inside = (col_frames >= 0) & (col_frames < FRAMES)
        valid = (distance[None, :, :] <= windows[:, None, None]) & inside[None, None, :]
        weights = masked_softmax(scores, valid)
        context = jnp.einsum('hqk,khd->qhd', weights.astype(jnp.float32), value_block)
        return context.astype(jnp.bfloat16)
    enc_context = lax.map(enc_block, jnp.arange(N_SEQ, dtype=jnp.int32)).reshape(FRAMES, EH * EHD)
    mixed = jnp.dot(enc_context, enc_wo, preferred_element_type=jnp.float32)
    enc_out = (audio.astype(jnp.float32) + mixed + enc_bo).astype(jnp.bfloat16)
    band_bias = jnp.concatenate([jnp.zeros_like(dec_bv), dec_bv], axis=1)
    band_kv = jnp.dot(enc_out, dec_wkv.reshape(D_ENC, KVG * 2 * HD), preferred_element_type=jnp.float32)
    band_kv = (band_kv.reshape(FRAMES, KVG, 2 * HD) + band_bias).astype(jnp.bfloat16)
    pad_band = jnp.pad(band_kv, ((BAND, BAND), (0, 0), (0, 0)))
    normed = rms_norm(text, norm_gain).astype(jnp.bfloat16)
    dec_query = (jnp.dot(normed, dec_wq, preferred_element_type=jnp.float32) + dec_bq).astype(jnp.bfloat16)
    dec_query = dec_query.reshape(ROWS, KVG, QPG, HD)
    band_extent = FR_SEQ + 2 * BAND
    set_width = GL * QPG * HD

    def dec_block(block_index):
        first_row = block_index * ROWS_DEV
        first_frame = block_index * FR_SEQ
        query_block = lax.dynamic_slice_in_dim(dec_query, first_row, ROWS_DEV, 0).astype(jnp.float32)
        pair_block = lax.dynamic_slice_in_dim(pad_band, first_frame, band_extent, 0).astype(jnp.float32)
        key_block = pair_block[:, :, :HD]
        value_block = pair_block[:, :, HD:]
        scores = jnp.einsum('rgqd,kgd->rgqk', query_block, key_block) * HD ** (-0.5)
        begins = lax.dynamic_slice_in_dim(span_start, first_row, ROWS_DEV, 0)
        counts = lax.dynamic_slice_in_dim(span_len, first_row, ROWS_DEV, 0)
        col_frames = first_frame - BAND + jnp.arange(band_extent, dtype=jnp.int32)
        valid = (col_frames[None, :] >= begins[:, None]) & (col_frames[None, :] < (begins + counts)[:, None])
        weights = masked_softmax(scores, valid[:, None, None, :])
        context = jnp.einsum('rgqk,kgd->rgqd', weights.astype(jnp.float32), value_block)
        context = context.astype(jnp.bfloat16).reshape(ROWS_DEV, KVG * QPG * HD)
        total = jnp.zeros((ROWS_DEV, D), jnp.float32)
        for head_set in range(N_HEADS):
            term = jnp.dot(context[:, head_set * set_width:(head_set + 1) * set_width], dec_wo[head_set * set_width:(head_set + 1) * set_width], preferred_element_type=jnp.float32)
            total = total + lax.optimization_barrier(term.astype(jnp.bfloat16)).astype(jnp.float32)
        text_block = lax.dynamic_slice_in_dim(text, first_row, ROWS_DEV, 0)
        return (text_block.astype(jnp.float32) + total).astype(jnp.bfloat16)
    dec_out = lax.map(dec_block, jnp.arange(N_SEQ, dtype=jnp.int32)).reshape(ROWS, D)
    return (enc_out, dec_out)
```

```python
import jax
import jax.numpy as jnp
from jax import lax
from jax.sharding import PartitionSpec as P

EWIN = 128
BAND = 256
SEQ_OUTER = 4


def with_halo(block, sides, width):
    for axis, dim in sides:
        count = lax.axis_size(axis)
        forward = [(i, i + 1) for i in range(count - 1)]
        backward = [(target, source) for source, target in forward]
        low = lax.ppermute(
            lax.slice_in_dim(block, block.shape[dim] - width, None, axis=dim), axis, forward
        )
        high = lax.ppermute(lax.slice_in_dim(block, 0, width, axis=dim), axis, backward)
        block = jnp.concatenate([low, block, high], axis=dim)
    return block


def ring_gather(piece, axis, stride, count, parts_dim):
    size = lax.axis_size(axis)
    def shifted(step):
        pairs = []
        for source in range(size):
            ring_pos = (source // stride) % count
            base = source - ring_pos * stride
            pairs.append((source, base + ((ring_pos + step) % count) * stride))
        return pairs
    from_behind = lax.ppermute(piece, axis, shifted(1))
    from_ahead = lax.ppermute(piece, axis, shifted(-1))
    half = piece.shape[parts_dim] // 2
    first = lax.ppermute(lax.slice_in_dim(from_behind, 0, half, axis=parts_dim), axis, shifted(1))
    second = lax.ppermute(lax.slice_in_dim(from_ahead, half, None, axis=parts_dim), axis, shifted(-1))
    opposite = jnp.concatenate([first, second], axis=parts_dim)
    return jnp.stack([piece, from_ahead, opposite, from_behind], axis=0)


def torus_gather(block, axis, outer, inner):
    rows = block.shape[0]
    half = rows // 2
    split_dim = 1
    first = ring_gather(block[:half], axis, 1, inner, split_dim)
    first = ring_gather(first, axis, inner, outer, split_dim + 1)
    second = ring_gather(block[half:], axis, inner, outer, split_dim)
    second = ring_gather(second, axis, 1, inner, split_dim + 1)
    second = jnp.swapaxes(second, 0, 1)
    merged = jnp.concatenate([first, second], axis=2)
    index = lax.axis_index(axis)
    merged = jnp.roll(merged, index // inner, axis=0)
    return jnp.roll(merged, index % inner, axis=1)


def layer_norm(values, gain, shift):
    values = values.astype(jnp.float32)
    centre = values - jnp.mean(values, axis=-1, keepdims=True)
    spread = jnp.mean(centre * centre, axis=-1, keepdims=True)
    return centre * lax.rsqrt(spread + 1e-05) * gain + shift


def rms_norm(values, gain):
    values = values.astype(jnp.float32)
    return values * lax.rsqrt(jnp.mean(values * values, axis=-1, keepdims=True) + 1e-06) * gain


def masked_softmax(scores, valid):
    highest = jnp.max(jnp.where(valid, scores, -jnp.inf), axis=-1, keepdims=True)
    raised = jnp.where(valid, jnp.exp(scores - highest), jnp.zeros_like(scores))
    return (raised / jnp.sum(raised, axis=-1, keepdims=True)).astype(jnp.bfloat16)


def shards(
    audio,
    ln_gain,
    ln_shift,
    enc_wq,
    enc_bq,
    enc_wk,
    enc_wv,
    enc_bv,
    enc_wo,
    enc_bo,
    windows,
    dec_wkv,
    dec_bv,
    text,
    norm_gain,
    dec_wq,
    dec_bq,
    dec_wo,
    span_start,
    span_len,
):
    seq_count = lax.axis_size("seq")
    head_count = lax.axis_size("heads")
    seq_index = lax.axis_index("seq")
    head_index = lax.axis_index("heads")
    frames_dev = audio.shape[0]
    enc_width = audio.shape[1]
    heads_dev = windows.shape[0]
    head_size = enc_wq.shape[1] // heads_dev
    all_frames = frames_dev * seq_count
    hidden = layer_norm(audio, ln_gain, ln_shift).astype(jnp.bfloat16)
    enc_query = (jnp.dot(hidden, enc_wq, preferred_element_type=jnp.float32) + enc_bq).astype(
        jnp.bfloat16
    )
    enc_keys = jnp.dot(hidden, enc_wk, preferred_element_type=jnp.float32).astype(jnp.bfloat16)
    enc_values = (jnp.dot(hidden, enc_wv, preferred_element_type=jnp.float32) + enc_bv).astype(
        jnp.bfloat16
    )
    enc_pairs = jnp.stack([enc_keys, enc_values], axis=1)
    widened = with_halo(enc_pairs, (("seq", 0),), EWIN)
    extent = frames_dev + 2 * EWIN
    key_block = widened[:, 0, :].reshape(extent, heads_dev, head_size)
    value_block = widened[:, 1, :].reshape(extent, heads_dev, head_size)
    query_block = enc_query.reshape(frames_dev, heads_dev, head_size)
    scores = jnp.einsum(
        "qhd,khd->hqk", query_block, key_block, preferred_element_type=jnp.float32
    ) * head_size ** (-0.5)
    row_frames = seq_index * frames_dev + jnp.arange(frames_dev, dtype=jnp.int32)
    col_frames = seq_index * frames_dev - EWIN + jnp.arange(extent, dtype=jnp.int32)
    distance = jnp.abs(row_frames[:, None] - col_frames[None, :])
    inside = (col_frames >= 0) & (col_frames < all_frames)
    valid = (distance[None, :, :] <= windows[:, None, None]) & inside[None, None, :]
    enc_weights = masked_softmax(scores, valid)
    enc_context = jnp.einsum(
        "hqk,khd->qhd", enc_weights, value_block, preferred_element_type=jnp.float32
    )
    enc_context = enc_context.astype(jnp.bfloat16).reshape(frames_dev, heads_dev * head_size)
    enc_term = jnp.dot(enc_context, enc_wo, preferred_element_type=jnp.float32)
    mixed = lax.psum_scatter(
        enc_term.astype(jnp.bfloat16), "heads", scatter_dimension=0, tiled=True
    ).astype(jnp.float32)
    share = frames_dev // head_count
    own_audio = lax.dynamic_slice_in_dim(audio, head_index * share, share, 0)
    enc_out = (own_audio.astype(jnp.float32) + mixed + enc_bo).astype(jnp.bfloat16)
    groups_dev = dec_wkv.shape[1] // head_count
    pair_width = dec_wkv.shape[2]
    dec_head = pair_width // 2
    band_bias = jnp.concatenate([jnp.zeros_like(dec_bv), dec_bv], axis=1)
    frames_all = lax.all_gather(enc_out, "heads", axis=0, tiled=True)
    weight_group = lax.dynamic_slice_in_dim(
        dec_wkv, head_index * groups_dev, groups_dev, 1
    ).reshape(enc_width, groups_dev * pair_width)
    bias_group = lax.dynamic_slice_in_dim(
        band_bias, head_index * groups_dev, groups_dev, 0
    ).reshape(groups_dev * pair_width)
    band_pairs = (
        jnp.dot(frames_all, weight_group, preferred_element_type=jnp.float32) + bias_group
    ).astype(jnp.bfloat16)
    band_pairs = band_pairs.reshape(frames_dev, groups_dev, pair_width)
    band_wide = with_halo(band_pairs, (("seq", 0),), BAND)
    rows_dev = text.shape[0]
    model_width = text.shape[1]
    query_width = dec_wq.shape[1]
    query_heads = query_width // (groups_dev * dec_head)
    normed = rms_norm(text, norm_gain).astype(jnp.bfloat16)
    query_sum = jnp.dot(
        normed,
        torus_gather(dec_wq, "seq", SEQ_OUTER, seq_count // SEQ_OUTER).reshape(
            seq_count * dec_wq.shape[0], dec_wq.shape[1]
        ),
        preferred_element_type=jnp.float32,
    )
    dec_query = (
        (query_sum + dec_bq)
        .astype(jnp.bfloat16)
        .reshape(rows_dev, groups_dev, query_heads, dec_head)
    )
    band_extent = band_wide.shape[0]
    band_keys = band_wide[:, :, :dec_head]
    band_values = band_wide[:, :, dec_head:]
    dec_scores = jnp.einsum(
        "rgqd,kgd->rgqk", dec_query, band_keys, preferred_element_type=jnp.float32
    ) * dec_head ** (-0.5)
    band_frames = seq_index * frames_dev - BAND + jnp.arange(band_extent, dtype=jnp.int32)
    in_band = (band_frames[None, :] >= span_start[:, None]) & (
        band_frames[None, :] < (span_start + span_len)[:, None]
    )
    dec_weights = masked_softmax(dec_scores, in_band[:, None, None, :])
    dec_context = jnp.einsum(
        "rgqk,kgd->rgqd", dec_weights, band_values, preferred_element_type=jnp.float32
    )
    dec_context = dec_context.astype(jnp.bfloat16).reshape(rows_dev, query_width)
    dec_term = jnp.dot(
        dec_context,
        jnp.moveaxis(
            torus_gather(jnp.swapaxes(dec_wo, 0, 1), "seq", SEQ_OUTER, seq_count // SEQ_OUTER), 3, 0
        ).reshape(dec_wo.shape[0], seq_count * dec_wo.shape[1]),
        preferred_element_type=jnp.float32,
    )
    summed = lax.psum_scatter(
        dec_term.astype(jnp.bfloat16), "heads", scatter_dimension=1, tiled=True
    ).astype(jnp.float32)
    col_share = model_width // head_count
    own_text = lax.dynamic_slice_in_dim(text, head_index * col_share, col_share, 1)
    dec_out = (own_text.astype(jnp.float32) + summed).astype(jnp.bfloat16)
    return (enc_out, dec_out)


def solution(mesh):
    return jax.shard_map(
        shards,
        mesh=mesh,
        in_specs=(
            P("seq", None),
            P(),
            P(),
            P(None, "heads"),
            P("heads"),
            P(None, "heads"),
            P(None, "heads"),
            P("heads"),
            P("heads", None),
            P(),
            P("heads"),
            P(),
            P(),
            P("seq", None),
            P(),
            P("seq", "heads"),
            P("heads"),
            P("heads", "seq"),
            P("seq"),
            P("seq"),
        ),
        out_specs=(P(("seq", "heads"), None), P("seq", "heads")),
        check_vma=False,
    )
```

```python
import jax
import jax.numpy as jnp
from jax import lax
from jax.sharding import PartitionSpec as P

EWIN = 128
BAND = 256


def with_halo(block, sides, width):
    for axis, dim in sides:
        count = lax.axis_size(axis)
        forward = [(i, i + 1) for i in range(count - 1)]
        backward = [(target, source) for source, target in forward]
        low = lax.ppermute(
            lax.slice_in_dim(block, block.shape[dim] - width, None, axis=dim), axis, forward
        )
        high = lax.ppermute(lax.slice_in_dim(block, 0, width, axis=dim), axis, backward)
        block = jnp.concatenate([low, block, high], axis=dim)
    return block


def layer_norm(values, gain, shift):
    values = values.astype(jnp.float32)
    centre = values - jnp.mean(values, axis=-1, keepdims=True)
    spread = jnp.mean(centre * centre, axis=-1, keepdims=True)
    return centre * lax.rsqrt(spread + 1e-05) * gain + shift


def rms_norm(values, gain):
    values = values.astype(jnp.float32)
    return values * lax.rsqrt(jnp.mean(values * values, axis=-1, keepdims=True) + 1e-06) * gain


def masked_softmax(scores, valid):
    highest = jnp.max(jnp.where(valid, scores, -jnp.inf), axis=-1, keepdims=True)
    raised = jnp.where(valid, jnp.exp(scores - highest), jnp.zeros_like(scores))
    return (raised / jnp.sum(raised, axis=-1, keepdims=True)).astype(jnp.bfloat16)


def layer_body(
    audio,
    ln_gain,
    ln_shift,
    enc_wq,
    enc_bq,
    enc_wk,
    enc_wv,
    enc_bv,
    enc_wo,
    enc_bo,
    windows,
    dec_wkv,
    dec_bv,
    text,
    norm_gain,
    dec_wq,
    dec_bq,
    dec_wo,
    span_start,
    span_len,
):
    seq_count = lax.axis_size("seq")
    head_count = lax.axis_size("heads")
    seq_index = lax.axis_index("seq")
    head_index = lax.axis_index("heads")
    frames_dev = audio.shape[0]
    enc_width = audio.shape[1]
    heads_dev = windows.shape[0]
    head_size = enc_wq.shape[1] // heads_dev
    all_frames = frames_dev * seq_count
    query_weight = lax.all_gather(dec_wq, "seq", axis=0, tiled=True)
    output_weight = lax.all_gather(dec_wo, "seq", axis=1, tiled=True)
    hidden = layer_norm(audio, ln_gain, ln_shift).astype(jnp.bfloat16)
    enc_query = (jnp.dot(hidden, enc_wq, preferred_element_type=jnp.float32) + enc_bq).astype(
        jnp.bfloat16
    )
    enc_keys = jnp.dot(hidden, enc_wk, preferred_element_type=jnp.float32).astype(jnp.bfloat16)
    enc_values = (jnp.dot(hidden, enc_wv, preferred_element_type=jnp.float32) + enc_bv).astype(
        jnp.bfloat16
    )
    enc_pairs = jnp.stack([enc_keys, enc_values], axis=1)
    widened = with_halo(enc_pairs, (("seq", 0),), EWIN)
    extent = frames_dev + 2 * EWIN
    key_block = widened[:, 0, :].reshape(extent, heads_dev, head_size)
    value_block = widened[:, 1, :].reshape(extent, heads_dev, head_size)
    query_block = enc_query.reshape(frames_dev, heads_dev, head_size)
    scores = jnp.einsum(
        "qhd,khd->hqk", query_block, key_block, preferred_element_type=jnp.float32
    ) * head_size ** (-0.5)
    row_frames = seq_index * frames_dev + jnp.arange(frames_dev, dtype=jnp.int32)
    col_frames = seq_index * frames_dev - EWIN + jnp.arange(extent, dtype=jnp.int32)
    distance = jnp.abs(row_frames[:, None] - col_frames[None, :])
    inside = (col_frames >= 0) & (col_frames < all_frames)
    valid = (distance[None, :, :] <= windows[:, None, None]) & inside[None, None, :]
    enc_weights = masked_softmax(scores, valid)
    enc_context = jnp.einsum(
        "hqk,khd->qhd", enc_weights, value_block, preferred_element_type=jnp.float32
    )
    enc_context = enc_context.astype(jnp.bfloat16).reshape(frames_dev, heads_dev * head_size)
    enc_term = jnp.dot(enc_context, enc_wo, preferred_element_type=jnp.float32)
    mixed = lax.psum_scatter(
        enc_term.astype(jnp.bfloat16), "heads", scatter_dimension=0, tiled=True
    ).astype(jnp.float32)
    share = frames_dev // head_count
    own_audio = lax.dynamic_slice_in_dim(audio, head_index * share, share, 0)
    enc_out = (own_audio.astype(jnp.float32) + mixed + enc_bo).astype(jnp.bfloat16)
    groups_dev = dec_wkv.shape[1] // head_count
    pair_width = dec_wkv.shape[2]
    dec_head = pair_width // 2
    band_bias = jnp.concatenate([jnp.zeros_like(dec_bv), dec_bv], axis=1)
    frames_all = lax.all_gather(enc_out, "heads", axis=0, tiled=True)
    weight_group = lax.dynamic_slice_in_dim(
        dec_wkv, head_index * groups_dev, groups_dev, 1
    ).reshape(enc_width, groups_dev * pair_width)
    bias_group = lax.dynamic_slice_in_dim(
        band_bias, head_index * groups_dev, groups_dev, 0
    ).reshape(groups_dev * pair_width)
    band_pairs = (
        jnp.dot(frames_all, weight_group, preferred_element_type=jnp.float32) + bias_group
    ).astype(jnp.bfloat16)
    band_pairs = band_pairs.reshape(frames_dev, groups_dev, pair_width)
    band_wide = with_halo(band_pairs, (("seq", 0),), BAND)
    rows_dev = text.shape[0]
    model_width = text.shape[1]
    query_width = dec_wq.shape[1]
    query_heads = query_width // (groups_dev * dec_head)
    normed = rms_norm(text, norm_gain).astype(jnp.bfloat16)
    query_sum = jnp.dot(
        normed,
        query_weight,
        preferred_element_type=jnp.float32,
    )
    dec_query = (
        (query_sum + dec_bq)
        .astype(jnp.bfloat16)
        .reshape(rows_dev, groups_dev, query_heads, dec_head)
    )
    band_extent = band_wide.shape[0]
    band_keys = band_wide[:, :, :dec_head]
    band_values = band_wide[:, :, dec_head:]
    dec_scores = jnp.einsum(
        "rgqd,kgd->rgqk", dec_query, band_keys, preferred_element_type=jnp.float32
    ) * dec_head ** (-0.5)
    band_frames = seq_index * frames_dev - BAND + jnp.arange(band_extent, dtype=jnp.int32)
    in_band = (band_frames[None, :] >= span_start[:, None]) & (
        band_frames[None, :] < (span_start + span_len)[:, None]
    )
    dec_weights = masked_softmax(dec_scores, in_band[:, None, None, :])
    dec_context = jnp.einsum(
        "rgqk,kgd->rgqd", dec_weights, band_values, preferred_element_type=jnp.float32
    )
    dec_context = dec_context.astype(jnp.bfloat16).reshape(rows_dev, query_width)
    dec_term = jnp.dot(
        dec_context,
        output_weight,
        preferred_element_type=jnp.float32,
    )
    summed = lax.psum_scatter(
        dec_term.astype(jnp.bfloat16), "heads", scatter_dimension=1, tiled=True
    ).astype(jnp.float32)
    col_share = model_width // head_count
    own_text = lax.dynamic_slice_in_dim(text, head_index * col_share, col_share, 1)
    dec_out = (own_text.astype(jnp.float32) + summed).astype(jnp.bfloat16)
    return (enc_out, dec_out)


def solution(mesh):
    return jax.shard_map(
        layer_body,
        mesh=mesh,
        in_specs=(
            P("seq", None),
            P(),
            P(),
            P(None, "heads"),
            P("heads"),
            P(None, "heads"),
            P(None, "heads"),
            P("heads"),
            P("heads", None),
            P(),
            P("heads"),
            P(),
            P(),
            P("seq", None),
            P(),
            P("seq", "heads"),
            P("heads"),
            P("heads", "seq"),
            P("seq"),
            P("seq"),
        ),
        out_specs=(P(("seq", "heads"), None), P("seq", "heads")),
        check_vma=False,
    )
```

```python
import jax
import jax.numpy as jnp
from jax import lax
from jax.sharding import PartitionSpec as P

EWIN = 128
BAND = 256


def with_halo(block, sides, width):
    for axis, dim in sides:
        count = lax.axis_size(axis)
        forward = [(i, i + 1) for i in range(count - 1)]
        backward = [(target, source) for source, target in forward]
        low = lax.ppermute(
            lax.slice_in_dim(block, block.shape[dim] - width, None, axis=dim), axis, forward
        )
        high = lax.ppermute(lax.slice_in_dim(block, 0, width, axis=dim), axis, backward)
        block = jnp.concatenate([low, block, high], axis=dim)
    return block


def heads_gather(block, axis):
    count = lax.axis_size(axis)
    index = lax.axis_index(axis)
    gathered = block[None]
    bit = 1
    while bit < count:
        other = lax.ppermute(gathered, axis, [(i, i ^ bit) for i in range(count)])
        upper = (index & bit) != 0
        gathered = jnp.where(
            upper,
            jnp.concatenate([other, gathered], axis=0),
            jnp.concatenate([gathered, other], axis=0),
        )
        bit *= 2
    return gathered


def layer_norm(values, gain, shift):
    values = values.astype(jnp.float32)
    centre = values - jnp.mean(values, axis=-1, keepdims=True)
    spread = jnp.mean(centre * centre, axis=-1, keepdims=True)
    return centre * lax.rsqrt(spread + 1e-05) * gain + shift


def rms_norm(values, gain):
    values = values.astype(jnp.float32)
    return values * lax.rsqrt(jnp.mean(values * values, axis=-1, keepdims=True) + 1e-06) * gain


def masked_softmax(scores, valid):
    highest = jnp.max(jnp.where(valid, scores, -jnp.inf), axis=-1, keepdims=True)
    raised = jnp.where(valid, jnp.exp(scores - highest), jnp.zeros_like(scores))
    return (raised / jnp.sum(raised, axis=-1, keepdims=True)).astype(jnp.bfloat16)


def shards(
    audio,
    ln_gain,
    ln_shift,
    enc_wq,
    enc_bq,
    enc_wk,
    enc_wv,
    enc_bv,
    enc_wo,
    enc_bo,
    windows,
    dec_wkv,
    dec_bv,
    text,
    norm_gain,
    dec_wq,
    dec_bq,
    dec_wo,
    span_start,
    span_len,
):
    seq_count = lax.axis_size("seq")
    head_count = lax.axis_size("heads")
    seq_index = lax.axis_index("seq")
    head_index = lax.axis_index("heads")
    frames_dev = audio.shape[0]
    enc_width = audio.shape[1]
    heads_dev = windows.shape[0]
    head_size = enc_wq.shape[1] // heads_dev
    all_frames = frames_dev * seq_count
    hidden = layer_norm(audio, ln_gain, ln_shift).astype(jnp.bfloat16)
    enc_query = (jnp.dot(hidden, enc_wq, preferred_element_type=jnp.float32) + enc_bq).astype(
        jnp.bfloat16
    )
    enc_keys = jnp.dot(hidden, enc_wk, preferred_element_type=jnp.float32).astype(jnp.bfloat16)
    enc_values = (jnp.dot(hidden, enc_wv, preferred_element_type=jnp.float32) + enc_bv).astype(
        jnp.bfloat16
    )
    enc_pairs = jnp.stack([enc_keys, enc_values], axis=1)
    widened = with_halo(enc_pairs, (("seq", 0),), EWIN)
    extent = frames_dev + 2 * EWIN
    key_block = widened[:, 0, :].reshape(extent, heads_dev, head_size)
    value_block = widened[:, 1, :].reshape(extent, heads_dev, head_size)
    query_block = enc_query.reshape(frames_dev, heads_dev, head_size)
    scores = jnp.einsum(
        "qhd,khd->hqk", query_block, key_block, preferred_element_type=jnp.float32
    ) * head_size ** (-0.5)
    row_frames = seq_index * frames_dev + jnp.arange(frames_dev, dtype=jnp.int32)
    col_frames = seq_index * frames_dev - EWIN + jnp.arange(extent, dtype=jnp.int32)
    distance = jnp.abs(row_frames[:, None] - col_frames[None, :])
    inside = (col_frames >= 0) & (col_frames < all_frames)
    valid = (distance[None, :, :] <= windows[:, None, None]) & inside[None, None, :]
    enc_weights = masked_softmax(scores, valid)
    enc_context = jnp.einsum(
        "hqk,khd->qhd", enc_weights, value_block, preferred_element_type=jnp.float32
    )
    enc_context = enc_context.astype(jnp.bfloat16).reshape(frames_dev, heads_dev * head_size)
    share = frames_dev // head_count
    full_wo = heads_gather(enc_wo, "heads").reshape(head_count * enc_wo.shape[0], enc_width)
    context_share = lax.all_to_all(enc_context, "heads", 0, 1, tiled=True)
    mixed = jnp.dot(context_share, full_wo, preferred_element_type=jnp.float32)
    own_audio = lax.dynamic_slice_in_dim(audio, head_index * share, share, 0)
    enc_out = (own_audio.astype(jnp.float32) + mixed + enc_bo).astype(jnp.bfloat16)
    groups = dec_wkv.shape[1]
    groups_dev = groups // head_count
    pair_width = dec_wkv.shape[2]
    dec_head = pair_width // 2
    band_bias = jnp.concatenate([jnp.zeros_like(dec_bv), dec_bv], axis=1)
    share_pairs = (
        jnp.dot(
            enc_out,
            dec_wkv.reshape(enc_width, groups * pair_width),
            preferred_element_type=jnp.float32,
        )
        + band_bias.reshape(groups * pair_width)
    ).astype(jnp.bfloat16)
    band_pairs = lax.all_to_all(share_pairs, "heads", 1, 0, tiled=True)
    band_pairs = band_pairs.reshape(frames_dev, groups_dev, pair_width)
    band_wide = with_halo(band_pairs, (("seq", 0),), BAND)
    rows_dev = text.shape[0]
    model_width = text.shape[1]
    query_width = dec_wq.shape[1]
    query_heads = query_width // (groups_dev * dec_head)
    normed = rms_norm(text, norm_gain).astype(jnp.bfloat16)
    query_sum = jnp.dot(
        normed,
        lax.all_gather(dec_wq, "seq", axis=0, tiled=True),
        preferred_element_type=jnp.float32,
    )
    dec_query = (
        (query_sum + dec_bq)
        .astype(jnp.bfloat16)
        .reshape(rows_dev, groups_dev, query_heads, dec_head)
    )
    band_extent = band_wide.shape[0]
    band_keys = band_wide[:, :, :dec_head]
    band_values = band_wide[:, :, dec_head:]
    dec_scores = jnp.einsum(
        "rgqd,kgd->rgqk", dec_query, band_keys, preferred_element_type=jnp.float32
    ) * dec_head ** (-0.5)
    band_frames = seq_index * frames_dev - BAND + jnp.arange(band_extent, dtype=jnp.int32)
    in_band = (band_frames[None, :] >= span_start[:, None]) & (
        band_frames[None, :] < (span_start + span_len)[:, None]
    )
    dec_weights = masked_softmax(dec_scores, in_band[:, None, None, :])
    dec_context = jnp.einsum(
        "rgqk,kgd->rgqd", dec_weights, band_values, preferred_element_type=jnp.float32
    )
    dec_context = dec_context.astype(jnp.bfloat16).reshape(rows_dev, query_width)
    dec_term = jnp.dot(
        dec_context,
        lax.all_gather(dec_wo, "seq", axis=1, tiled=True),
        preferred_element_type=jnp.float32,
    )
    summed = lax.psum_scatter(
        dec_term.astype(jnp.bfloat16), "heads", scatter_dimension=1, tiled=True
    ).astype(jnp.float32)
    col_share = model_width // head_count
    own_text = lax.dynamic_slice_in_dim(text, head_index * col_share, col_share, 1)
    dec_out = (own_text.astype(jnp.float32) + summed).astype(jnp.bfloat16)
    return (enc_out, dec_out)


def solution(mesh):
    return jax.shard_map(
        shards,
        mesh=mesh,
        in_specs=(
            P("seq", None),
            P(),
            P(),
            P(None, "heads"),
            P("heads"),
            P(None, "heads"),
            P(None, "heads"),
            P("heads"),
            P("heads", None),
            P(),
            P("heads"),
            P(),
            P(),
            P("seq", None),
            P(),
            P("seq", "heads"),
            P("heads"),
            P("heads", "seq"),
            P("seq"),
            P("seq"),
        ),
        out_specs=(P(("seq", "heads"), None), P("seq", "heads")),
        check_vma=False,
    )
```

```python
import jax
import jax.numpy as jnp
from jax import lax
from jax.sharding import PartitionSpec as P

EWIN = 128
BAND = 256


def with_halo(block, sides, width):
    for axis, dim in sides:
        count = lax.axis_size(axis)
        forward = [(i, i + 1) for i in range(count - 1)]
        backward = [(target, source) for source, target in forward]
        low = lax.ppermute(
            lax.slice_in_dim(block, block.shape[dim] - width, None, axis=dim), axis, forward
        )
        high = lax.ppermute(lax.slice_in_dim(block, 0, width, axis=dim), axis, backward)
        block = jnp.concatenate([low, block, high], axis=dim)
    return block


def heads_gather(block, axis):
    count = lax.axis_size(axis)
    index = lax.axis_index(axis)
    gathered = block[None]
    bit = 1
    while bit < count:
        other = lax.ppermute(gathered, axis, [(i, i ^ bit) for i in range(count)])
        upper = (index & bit) != 0
        gathered = jnp.where(
            upper,
            jnp.concatenate([other, gathered], axis=0),
            jnp.concatenate([gathered, other], axis=0),
        )
        bit *= 2
    return gathered


def layer_norm(values, gain, shift):
    values = values.astype(jnp.float32)
    centre = values - jnp.mean(values, axis=-1, keepdims=True)
    spread = jnp.mean(centre * centre, axis=-1, keepdims=True)
    return centre * lax.rsqrt(spread + 1e-05) * gain + shift


def rms_norm(values, gain):
    values = values.astype(jnp.float32)
    return values * lax.rsqrt(jnp.mean(values * values, axis=-1, keepdims=True) + 1e-06) * gain


def masked_softmax(scores, valid):
    highest = jnp.max(jnp.where(valid, scores, -jnp.inf), axis=-1, keepdims=True)
    raised = jnp.where(valid, jnp.exp(scores - highest), jnp.zeros_like(scores))
    return (raised / jnp.sum(raised, axis=-1, keepdims=True)).astype(jnp.bfloat16)


def layer_body(
    audio,
    ln_gain,
    ln_shift,
    enc_wq,
    enc_bq,
    enc_wk,
    enc_wv,
    enc_bv,
    enc_wo,
    enc_bo,
    windows,
    dec_wkv,
    dec_bv,
    text,
    norm_gain,
    dec_wq,
    dec_bq,
    dec_wo,
    span_start,
    span_len,
):
    seq_count = lax.axis_size("seq")
    head_count = lax.axis_size("heads")
    seq_index = lax.axis_index("seq")
    head_index = lax.axis_index("heads")
    frames_dev = audio.shape[0]
    enc_width = audio.shape[1]
    heads_dev = windows.shape[0]
    head_size = enc_wq.shape[1] // heads_dev
    all_frames = frames_dev * seq_count
    output_weight = lax.all_to_all(jnp.tile(dec_wo, (1, seq_count)), "seq", 1, 1, tiled=True)
    hidden = layer_norm(audio, ln_gain, ln_shift).astype(jnp.bfloat16)
    enc_query = (jnp.dot(hidden, enc_wq, preferred_element_type=jnp.float32) + enc_bq).astype(
        jnp.bfloat16
    )
    enc_keys = jnp.dot(hidden, enc_wk, preferred_element_type=jnp.float32).astype(jnp.bfloat16)
    enc_values = (jnp.dot(hidden, enc_wv, preferred_element_type=jnp.float32) + enc_bv).astype(
        jnp.bfloat16
    )
    enc_pairs = jnp.stack([enc_keys, enc_values], axis=1)
    widened = with_halo(enc_pairs, (("seq", 0),), EWIN)
    extent = frames_dev + 2 * EWIN
    key_block = widened[:, 0, :].reshape(extent, heads_dev, head_size)
    value_block = widened[:, 1, :].reshape(extent, heads_dev, head_size)
    query_block = enc_query.reshape(frames_dev, heads_dev, head_size)
    scores = jnp.einsum(
        "qhd,khd->hqk", query_block, key_block, preferred_element_type=jnp.float32
    ) * head_size ** (-0.5)
    row_frames = seq_index * frames_dev + jnp.arange(frames_dev, dtype=jnp.int32)
    col_frames = seq_index * frames_dev - EWIN + jnp.arange(extent, dtype=jnp.int32)
    distance = jnp.abs(row_frames[:, None] - col_frames[None, :])
    inside = (col_frames >= 0) & (col_frames < all_frames)
    valid = (distance[None, :, :] <= windows[:, None, None]) & inside[None, None, :]
    enc_weights = masked_softmax(scores, valid)
    enc_context = jnp.einsum(
        "hqk,khd->qhd", enc_weights, value_block, preferred_element_type=jnp.float32
    )
    enc_context = enc_context.astype(jnp.bfloat16).reshape(frames_dev, heads_dev * head_size)
    share = frames_dev // head_count
    full_wo = heads_gather(enc_wo, "heads").reshape(head_count * enc_wo.shape[0], enc_width)
    context_all = heads_gather(enc_context.reshape(head_count, share, enc_context.shape[1]), "heads")
    context_share = lax.dynamic_index_in_dim(
        jnp.moveaxis(context_all, 0, 2), head_index, 0, keepdims=False
    ).reshape(share, head_count * enc_context.shape[1])
    mixed = jnp.dot(context_share, full_wo, preferred_element_type=jnp.float32)
    own_audio = lax.dynamic_slice_in_dim(audio, head_index * share, share, 0)
    enc_out = (own_audio.astype(jnp.float32) + mixed + enc_bo).astype(jnp.bfloat16)
    groups = dec_wkv.shape[1]
    groups_dev = groups // head_count
    pair_width = dec_wkv.shape[2]
    dec_head = pair_width // 2
    band_bias = jnp.concatenate([jnp.zeros_like(dec_bv), dec_bv], axis=1)
    frames_all = heads_gather(enc_out, "heads").reshape(frames_dev, enc_width)
    weight_group = lax.dynamic_slice_in_dim(
        dec_wkv, head_index * groups_dev, groups_dev, 1
    ).reshape(enc_width, groups_dev * pair_width)
    bias_group = lax.dynamic_slice_in_dim(
        band_bias, head_index * groups_dev, groups_dev, 0
    ).reshape(groups_dev * pair_width)
    band_pairs = (
        jnp.dot(frames_all, weight_group, preferred_element_type=jnp.float32) + bias_group
    ).astype(jnp.bfloat16)
    band_pairs = band_pairs.reshape(frames_dev, groups_dev, pair_width)
    band_wide = with_halo(band_pairs, (("seq", 0),), BAND)
    rows_dev = text.shape[0]
    model_width = text.shape[1]
    query_width = dec_wq.shape[1]
    query_heads = query_width // (groups_dev * dec_head)
    normed = rms_norm(text, norm_gain).astype(jnp.bfloat16)
    query_sum = jnp.dot(
        normed,
        lax.all_gather(dec_wq, "seq", axis=0, tiled=True),
        preferred_element_type=jnp.float32,
    )
    dec_query = (
        (query_sum + dec_bq)
        .astype(jnp.bfloat16)
        .reshape(rows_dev, groups_dev, query_heads, dec_head)
    )
    band_extent = band_wide.shape[0]
    band_keys = band_wide[:, :, :dec_head]
    band_values = band_wide[:, :, dec_head:]
    dec_scores = jnp.einsum(
        "rgqd,kgd->rgqk", dec_query, band_keys, preferred_element_type=jnp.float32
    ) * dec_head ** (-0.5)
    band_frames = seq_index * frames_dev - BAND + jnp.arange(band_extent, dtype=jnp.int32)
    in_band = (band_frames[None, :] >= span_start[:, None]) & (
        band_frames[None, :] < (span_start + span_len)[:, None]
    )
    dec_weights = masked_softmax(dec_scores, in_band[:, None, None, :])
    dec_context = jnp.einsum(
        "rgqk,kgd->rgqd", dec_weights, band_values, preferred_element_type=jnp.float32
    )
    dec_context = dec_context.astype(jnp.bfloat16).reshape(rows_dev, query_width)
    dec_term = jnp.dot(
        dec_context,
        output_weight,
        preferred_element_type=jnp.float32,
    )
    summed = lax.psum_scatter(
        dec_term.astype(jnp.bfloat16), "heads", scatter_dimension=1, tiled=True
    ).astype(jnp.float32)
    col_share = model_width // head_count
    own_text = lax.dynamic_slice_in_dim(text, head_index * col_share, col_share, 1)
    dec_out = (own_text.astype(jnp.float32) + summed).astype(jnp.bfloat16)
    return (enc_out, dec_out)


def solution(mesh):
    return jax.shard_map(
        layer_body,
        mesh=mesh,
        in_specs=(
            P("seq", None),
            P(),
            P(),
            P(None, "heads"),
            P("heads"),
            P(None, "heads"),
            P(None, "heads"),
            P("heads"),
            P("heads", None),
            P(),
            P("heads"),
            P(),
            P(),
            P("seq", None),
            P(),
            P("seq", "heads"),
            P("heads"),
            P("heads", "seq"),
            P("seq"),
            P("seq"),
        ),
        out_specs=(P(("seq", "heads"), None), P("seq", "heads")),
        check_vma=False,
    )
```

```python
import jax
import jax.numpy as jnp
from jax import lax
from jax.sharding import PartitionSpec as P

EWIN = 128
BAND = 256


def with_halo(block, sides, width):
    for axis, dim in sides:
        count = lax.axis_size(axis)
        forward = [(i, i + 1) for i in range(count - 1)]
        backward = [(target, source) for source, target in forward]
        low = lax.ppermute(
            lax.slice_in_dim(block, block.shape[dim] - width, None, axis=dim), axis, forward
        )
        high = lax.ppermute(lax.slice_in_dim(block, 0, width, axis=dim), axis, backward)
        block = jnp.concatenate([low, block, high], axis=dim)
    return block


def heads_gather(block, axis):
    count = lax.axis_size(axis)
    index = lax.axis_index(axis)
    gathered = block[None]
    bit = 1
    while bit < count:
        other = lax.ppermute(gathered, axis, [(i, i ^ bit) for i in range(count)])
        upper = (index & bit) != 0
        gathered = jnp.where(
            upper,
            jnp.concatenate([other, gathered], axis=0),
            jnp.concatenate([gathered, other], axis=0),
        )
        bit *= 2
    return gathered


def heads_ring_gather(block, axis):
    count = lax.axis_size(axis)
    ring = count // 2
    index = lax.axis_index(axis)
    chip = index // 2
    core = index % 2
    swap = [(i, i ^ 1) for i in range(count)]
    sibling = lax.ppermute(block, axis, swap)
    own = jnp.where(core == 0, jnp.stack([block, sibling]), jnp.stack([sibling, block]))
    step = []
    for i in range(count):
        direction = 1 if i % 2 == 0 else -1
        step.append((i, ((i // 2 + direction) % ring) * 2 + i % 2))
    near = lax.ppermute(own, axis, step)
    far = lax.ppermute(near, axis, step)
    other = lax.ppermute(near, axis, swap)
    sign = 1 - 2 * core
    owners = [chip, (chip - sign) % ring, (chip + 2) % ring, (chip + sign) % ring]
    return [own, near, far, other], owners


def layer_norm(values, gain, shift):
    values = values.astype(jnp.float32)
    centre = values - jnp.mean(values, axis=-1, keepdims=True)
    spread = jnp.mean(centre * centre, axis=-1, keepdims=True)
    return centre * lax.rsqrt(spread + 1e-05) * gain + shift


def rms_norm(values, gain):
    values = values.astype(jnp.float32)
    return values * lax.rsqrt(jnp.mean(values * values, axis=-1, keepdims=True) + 1e-06) * gain


def masked_softmax(scores, valid):
    highest = jnp.max(jnp.where(valid, scores, -jnp.inf), axis=-1, keepdims=True)
    raised = jnp.where(valid, jnp.exp(scores - highest), jnp.zeros_like(scores))
    return (raised / jnp.sum(raised, axis=-1, keepdims=True)).astype(jnp.bfloat16)


def shards(
    audio,
    ln_gain,
    ln_shift,
    enc_wq,
    enc_bq,
    enc_wk,
    enc_wv,
    enc_bv,
    enc_wo,
    enc_bo,
    windows,
    dec_wkv,
    dec_bv,
    text,
    norm_gain,
    dec_wq,
    dec_bq,
    dec_wo,
    span_start,
    span_len,
):
    seq_count = lax.axis_size("seq")
    head_count = lax.axis_size("heads")
    seq_index = lax.axis_index("seq")
    head_index = lax.axis_index("heads")
    frames_dev = audio.shape[0]
    enc_width = audio.shape[1]
    heads_dev = windows.shape[0]
    head_size = enc_wq.shape[1] // heads_dev
    all_frames = frames_dev * seq_count
    hidden = layer_norm(audio, ln_gain, ln_shift).astype(jnp.bfloat16)
    enc_query = (jnp.dot(hidden, enc_wq, preferred_element_type=jnp.float32) + enc_bq).astype(
        jnp.bfloat16
    )
    enc_keys = jnp.dot(hidden, enc_wk, preferred_element_type=jnp.float32).astype(jnp.bfloat16)
    enc_values = (jnp.dot(hidden, enc_wv, preferred_element_type=jnp.float32) + enc_bv).astype(
        jnp.bfloat16
    )
    enc_pairs = jnp.stack([enc_keys, enc_values], axis=1)
    widened = with_halo(enc_pairs, (("seq", 0),), EWIN)
    extent = frames_dev + 2 * EWIN
    key_block = widened[:, 0, :].reshape(extent, heads_dev, head_size)
    value_block = widened[:, 1, :].reshape(extent, heads_dev, head_size)
    query_block = enc_query.reshape(frames_dev, heads_dev, head_size)
    scores = jnp.einsum(
        "qhd,khd->hqk", query_block, key_block, preferred_element_type=jnp.float32
    ) * head_size ** (-0.5)
    row_frames = seq_index * frames_dev + jnp.arange(frames_dev, dtype=jnp.int32)
    col_frames = seq_index * frames_dev - EWIN + jnp.arange(extent, dtype=jnp.int32)
    distance = jnp.abs(row_frames[:, None] - col_frames[None, :])
    inside = (col_frames >= 0) & (col_frames < all_frames)
    valid = (distance[None, :, :] <= windows[:, None, None]) & inside[None, None, :]
    enc_weights = masked_softmax(scores, valid)
    enc_context = jnp.einsum(
        "hqk,khd->qhd", enc_weights, value_block, preferred_element_type=jnp.float32
    )
    enc_context = enc_context.astype(jnp.bfloat16).reshape(frames_dev, heads_dev * head_size)
    share = frames_dev // head_count
    full_wo = heads_gather(enc_wo, "heads").reshape(head_count * enc_wo.shape[0], enc_width)
    context_share = lax.all_to_all(enc_context, "heads", 0, 1, tiled=True)
    mixed = jnp.dot(context_share, full_wo, preferred_element_type=jnp.float32)
    own_audio = lax.dynamic_slice_in_dim(audio, head_index * share, share, 0)
    enc_out = (own_audio.astype(jnp.float32) + mixed + enc_bo).astype(jnp.bfloat16)
    groups = dec_wkv.shape[1]
    groups_dev = groups // head_count
    pair_width = dec_wkv.shape[2]
    dec_head = pair_width // 2
    band_bias = jnp.concatenate([jnp.zeros_like(dec_bv), dec_bv], axis=1)
    share_pairs = (
        jnp.dot(
            enc_out,
            dec_wkv.reshape(enc_width, groups * pair_width),
            preferred_element_type=jnp.float32,
        )
        + band_bias.reshape(groups * pair_width)
    ).astype(jnp.bfloat16)
    band_pairs = lax.all_to_all(share_pairs, "heads", 1, 0, tiled=True)
    band_pairs = band_pairs.reshape(frames_dev, groups_dev, pair_width)
    band_wide = with_halo(band_pairs, (("seq", 0),), BAND)
    rows_dev = text.shape[0]
    model_width = text.shape[1]
    query_width = dec_wq.shape[1]
    query_heads = query_width // (groups_dev * dec_head)
    normed = rms_norm(text, norm_gain).astype(jnp.bfloat16)
    query_sum = jnp.dot(
        normed,
        lax.all_gather(dec_wq, "seq", axis=0, tiled=True),
        preferred_element_type=jnp.float32,
    )
    dec_query = (
        (query_sum + dec_bq)
        .astype(jnp.bfloat16)
        .reshape(rows_dev, groups_dev, query_heads, dec_head)
    )
    band_extent = band_wide.shape[0]
    band_keys = band_wide[:, :, :dec_head]
    band_values = band_wide[:, :, dec_head:]
    dec_scores = jnp.einsum(
        "rgqd,kgd->rgqk", dec_query, band_keys, preferred_element_type=jnp.float32
    ) * dec_head ** (-0.5)
    band_frames = seq_index * frames_dev - BAND + jnp.arange(band_extent, dtype=jnp.int32)
    in_band = (band_frames[None, :] >= span_start[:, None]) & (
        band_frames[None, :] < (span_start + span_len)[:, None]
    )
    dec_weights = masked_softmax(dec_scores, in_band[:, None, None, :])
    dec_context = jnp.einsum(
        "rgqk,kgd->rgqd", dec_weights, band_values, preferred_element_type=jnp.float32
    )
    dec_context = dec_context.astype(jnp.bfloat16).reshape(rows_dev, query_width)
    ratio = seq_count // head_count
    set_rows = dec_wo.shape[0]
    block_cols = dec_wo.shape[1]
    flat = [(c, j) for c in range(seq_count) for j in range(head_count)]
    regroup = [
        (c * head_count + j, (ratio * j + c % ratio) * head_count + c // ratio) for c, j in flat
    ]
    piece = lax.ppermute(dec_wo, ("seq", "heads"), regroup)
    column_weight = lax.all_gather(piece, "seq", axis=0, tiled=False).reshape(
        head_count, ratio, set_rows, block_cols
    )
    pieces, owners = heads_ring_gather(dec_context, "heads")
    total = jnp.zeros((rows_dev, ratio, block_cols), jnp.float32)
    for held, owner in zip(pieces, owners):
        for offset in range(held.shape[0]):
            weight_set = lax.dynamic_index_in_dim(
                column_weight, owner * held.shape[0] + offset, 0, keepdims=False
            )
            term = jnp.einsum(
                "rk,bkc->rbc", held[offset], weight_set, preferred_element_type=jnp.float32
            )
            total = total + term.astype(jnp.bfloat16).astype(jnp.float32)
    summed = total.reshape(rows_dev, ratio * block_cols)
    col_share = model_width // head_count
    own_text = lax.dynamic_slice_in_dim(text, head_index * col_share, col_share, 1)
    dec_out = (own_text.astype(jnp.float32) + summed).astype(jnp.bfloat16)
    return (enc_out, dec_out)


def solution(mesh):
    return jax.shard_map(
        shards,
        mesh=mesh,
        in_specs=(
            P("seq", None),
            P(),
            P(),
            P(None, "heads"),
            P("heads"),
            P(None, "heads"),
            P(None, "heads"),
            P("heads"),
            P("heads", None),
            P(),
            P("heads"),
            P(),
            P(),
            P("seq", None),
            P(),
            P("seq", "heads"),
            P("heads"),
            P("heads", "seq"),
            P("seq"),
            P("seq"),
        ),
        out_specs=(P(("seq", "heads"), None), P("seq", "heads")),
        check_vma=False,
    )
```

```python
import jax
import jax.numpy as jnp
from jax import lax
from jax.sharding import PartitionSpec as P

EWIN = 128
BAND = 256


def with_halo(block, sides, width):
    for axis, dim in sides:
        count = lax.axis_size(axis)
        forward = [(i, i + 1) for i in range(count - 1)]
        backward = [(target, source) for source, target in forward]
        low = lax.ppermute(
            lax.slice_in_dim(block, block.shape[dim] - width, None, axis=dim), axis, forward
        )
        high = lax.ppermute(lax.slice_in_dim(block, 0, width, axis=dim), axis, backward)
        block = jnp.concatenate([low, block, high], axis=dim)
    return block


def heads_gather(block, axis):
    count = lax.axis_size(axis)
    index = lax.axis_index(axis)
    gathered = block[None]
    bit = 1
    while bit < count:
        other = lax.ppermute(gathered, axis, [(i, i ^ bit) for i in range(count)])
        upper = (index & bit) != 0
        gathered = jnp.where(
            upper,
            jnp.concatenate([other, gathered], axis=0),
            jnp.concatenate([gathered, other], axis=0),
        )
        bit *= 2
    return gathered


def heads_ring_gather(block, axis):
    count = lax.axis_size(axis)
    ring = count // 2
    index = lax.axis_index(axis)
    chip = index // 2
    core = index % 2
    swap = [(i, i ^ 1) for i in range(count)]
    sibling = lax.ppermute(block, axis, swap)
    own = jnp.where(core == 0, jnp.stack([block, sibling]), jnp.stack([sibling, block]))
    step = []
    for i in range(count):
        direction = 1 if i % 2 == 0 else -1
        step.append((i, ((i // 2 + direction) % ring) * 2 + i % 2))
    near = lax.ppermute(own, axis, step)
    far = lax.ppermute(near, axis, step)
    other = lax.ppermute(near, axis, swap)
    sign = 1 - 2 * core
    owners = [chip, (chip - sign) % ring, (chip + 2) % ring, (chip + sign) % ring]
    return [own, near, far, other], owners


def layer_norm(values, gain, shift):
    values = values.astype(jnp.float32)
    centre = values - jnp.mean(values, axis=-1, keepdims=True)
    spread = jnp.mean(centre * centre, axis=-1, keepdims=True)
    return centre * lax.rsqrt(spread + 1e-05) * gain + shift


def rms_norm(values, gain):
    values = values.astype(jnp.float32)
    return values * lax.rsqrt(jnp.mean(values * values, axis=-1, keepdims=True) + 1e-06) * gain


def masked_softmax(scores, valid):
    highest = jnp.max(jnp.where(valid, scores, -jnp.inf), axis=-1, keepdims=True)
    raised = jnp.where(valid, jnp.exp(scores - highest), jnp.zeros_like(scores))
    return (raised / jnp.sum(raised, axis=-1, keepdims=True)).astype(jnp.bfloat16)


def shards(
    audio,
    ln_gain,
    ln_shift,
    enc_wq,
    enc_bq,
    enc_wk,
    enc_wv,
    enc_bv,
    enc_wo,
    enc_bo,
    windows,
    dec_wkv,
    dec_bv,
    text,
    norm_gain,
    dec_wq,
    dec_bq,
    dec_wo,
    span_start,
    span_len,
):
    seq_count = lax.axis_size("seq")
    head_count = lax.axis_size("heads")
    seq_index = lax.axis_index("seq")
    head_index = lax.axis_index("heads")
    frames_dev = audio.shape[0]
    enc_width = audio.shape[1]
    heads_dev = windows.shape[0]
    head_size = enc_wq.shape[1] // heads_dev
    all_frames = frames_dev * seq_count
    hidden = layer_norm(audio, ln_gain, ln_shift).astype(jnp.bfloat16)
    enc_query = (jnp.dot(hidden, enc_wq, preferred_element_type=jnp.float32) + enc_bq).astype(
        jnp.bfloat16
    )
    enc_keys = jnp.dot(hidden, enc_wk, preferred_element_type=jnp.float32).astype(jnp.bfloat16)
    enc_values = (jnp.dot(hidden, enc_wv, preferred_element_type=jnp.float32) + enc_bv).astype(
        jnp.bfloat16
    )
    enc_pairs = jnp.stack([enc_keys, enc_values], axis=1)
    widened = with_halo(enc_pairs, (("seq", 0),), EWIN)
    extent = frames_dev + 2 * EWIN
    key_block = widened[:, 0, :].reshape(extent, heads_dev, head_size)
    value_block = widened[:, 1, :].reshape(extent, heads_dev, head_size)
    query_block = enc_query.reshape(frames_dev, heads_dev, head_size)
    scores = jnp.einsum(
        "qhd,khd->hqk", query_block, key_block, preferred_element_type=jnp.float32
    ) * head_size ** (-0.5)
    row_frames = seq_index * frames_dev + jnp.arange(frames_dev, dtype=jnp.int32)
    col_frames = seq_index * frames_dev - EWIN + jnp.arange(extent, dtype=jnp.int32)
    distance = jnp.abs(row_frames[:, None] - col_frames[None, :])
    inside = (col_frames >= 0) & (col_frames < all_frames)
    valid = (distance[None, :, :] <= windows[:, None, None]) & inside[None, None, :]
    enc_weights = masked_softmax(scores, valid)
    enc_context = jnp.einsum(
        "hqk,khd->qhd", enc_weights, value_block, preferred_element_type=jnp.float32
    )
    enc_context = enc_context.astype(jnp.bfloat16).reshape(frames_dev, heads_dev * head_size)
    share = frames_dev // head_count
    enc_term = jnp.dot(enc_context, enc_wo, preferred_element_type=jnp.float32)
    mixed = jnp.sum(
        lax.all_to_all(
            enc_term.reshape(head_count, share, enc_width), "heads", 0, 0, tiled=True
        ),
        axis=0,
    )
    own_audio = lax.dynamic_slice_in_dim(audio, head_index * share, share, 0)
    enc_out = (own_audio.astype(jnp.float32) + mixed + enc_bo).astype(jnp.bfloat16)
    groups = dec_wkv.shape[1]
    groups_dev = groups // head_count
    pair_width = dec_wkv.shape[2]
    dec_head = pair_width // 2
    band_bias = jnp.concatenate([jnp.zeros_like(dec_bv), dec_bv], axis=1)
    share_pairs = (
        jnp.dot(
            enc_out,
            dec_wkv.reshape(enc_width, groups * pair_width),
            preferred_element_type=jnp.float32,
        )
        + band_bias.reshape(groups * pair_width)
    ).astype(jnp.bfloat16)
    band_pairs = lax.all_to_all(share_pairs, "heads", 1, 0, tiled=True)
    band_pairs = band_pairs.reshape(frames_dev, groups_dev, pair_width)
    band_wide = with_halo(band_pairs, (("seq", 0),), BAND)
    rows_dev = text.shape[0]
    model_width = text.shape[1]
    query_width = dec_wq.shape[1]
    query_heads = query_width // (groups_dev * dec_head)
    normed = rms_norm(text, norm_gain).astype(jnp.bfloat16)
    query_sum = jnp.dot(
        normed,
        lax.all_gather(dec_wq, "seq", axis=0, tiled=True),
        preferred_element_type=jnp.float32,
    )
    dec_query = (
        (query_sum + dec_bq)
        .astype(jnp.bfloat16)
        .reshape(rows_dev, groups_dev, query_heads, dec_head)
    )
    band_extent = band_wide.shape[0]
    band_keys = band_wide[:, :, :dec_head]
    band_values = band_wide[:, :, dec_head:]
    dec_scores = jnp.einsum(
        "rgqd,kgd->rgqk", dec_query, band_keys, preferred_element_type=jnp.float32
    ) * dec_head ** (-0.5)
    band_frames = seq_index * frames_dev - BAND + jnp.arange(band_extent, dtype=jnp.int32)
    in_band = (band_frames[None, :] >= span_start[:, None]) & (
        band_frames[None, :] < (span_start + span_len)[:, None]
    )
    dec_weights = masked_softmax(dec_scores, in_band[:, None, None, :])
    dec_context = jnp.einsum(
        "rgqk,kgd->rgqd", dec_weights, band_values, preferred_element_type=jnp.float32
    )
    dec_context = dec_context.astype(jnp.bfloat16).reshape(rows_dev, query_width)
    ratio = seq_count // head_count
    set_rows = dec_wo.shape[0]
    block_cols = dec_wo.shape[1]
    flat = [(c, j) for c in range(seq_count) for j in range(head_count)]
    regroup = [
        (c * head_count + j, (ratio * j + c % ratio) * head_count + c // ratio) for c, j in flat
    ]
    piece = lax.ppermute(dec_wo, ("seq", "heads"), regroup)
    column_weight = lax.all_gather(piece, "seq", axis=0, tiled=False).reshape(
        head_count, ratio, set_rows, block_cols
    )
    pieces, owners = heads_ring_gather(dec_context, "heads")
    total = jnp.zeros((rows_dev, ratio, block_cols), jnp.float32)
    for held, owner in zip(pieces, owners):
        for offset in range(held.shape[0]):
            weight_set = lax.dynamic_index_in_dim(
                column_weight, owner * held.shape[0] + offset, 0, keepdims=False
            )
            term = jnp.einsum(
                "rk,bkc->rbc", held[offset], weight_set, preferred_element_type=jnp.float32
            )
            total = total + term.astype(jnp.bfloat16).astype(jnp.float32)
    summed = total.reshape(rows_dev, ratio * block_cols)
    col_share = model_width // head_count
    own_text = lax.dynamic_slice_in_dim(text, head_index * col_share, col_share, 1)
    dec_out = (own_text.astype(jnp.float32) + summed).astype(jnp.bfloat16)
    return (enc_out, dec_out)


def solution(mesh):
    return jax.shard_map(
        shards,
        mesh=mesh,
        in_specs=(
            P("seq", None),
            P(),
            P(),
            P(None, "heads"),
            P("heads"),
            P(None, "heads"),
            P(None, "heads"),
            P("heads"),
            P("heads", None),
            P(),
            P("heads"),
            P(),
            P(),
            P("seq", None),
            P(),
            P("seq", "heads"),
            P("heads"),
            P("heads", "seq"),
            P("seq"),
            P("seq"),
        ),
        out_specs=(P(("seq", "heads"), None), P("seq", "heads")),
        check_vma=False,
    )
```

```python
import jax
import jax.numpy as jnp
from jax import lax
from jax.sharding import PartitionSpec as P

EWIN = 128
BAND = 256


def with_halo(block, sides, width):
    for axis, dim in sides:
        count = lax.axis_size(axis)
        forward = [(i, i + 1) for i in range(count - 1)]
        backward = [(target, source) for source, target in forward]
        low = lax.ppermute(
            lax.slice_in_dim(block, block.shape[dim] - width, None, axis=dim), axis, forward
        )
        high = lax.ppermute(lax.slice_in_dim(block, 0, width, axis=dim), axis, backward)
        block = jnp.concatenate([low, block, high], axis=dim)
    return block


def heads_gather(block, axis):
    count = lax.axis_size(axis)
    index = lax.axis_index(axis)
    gathered = block[None]
    bit = 1
    while bit < count:
        other = lax.ppermute(gathered, axis, [(i, i ^ bit) for i in range(count)])
        upper = (index & bit) != 0
        gathered = jnp.where(
            upper,
            jnp.concatenate([other, gathered], axis=0),
            jnp.concatenate([gathered, other], axis=0),
        )
        bit *= 2
    return gathered


def heads_ring_gather(block, axis):
    count = lax.axis_size(axis)
    ring = count // 2
    index = lax.axis_index(axis)
    chip = index // 2
    core = index % 2
    swap = [(i, i ^ 1) for i in range(count)]
    sibling = lax.ppermute(block, axis, swap)
    own = jnp.where(core == 0, jnp.stack([block, sibling]), jnp.stack([sibling, block]))
    step = []
    for i in range(count):
        direction = 1 if i % 2 == 0 else -1
        step.append((i, ((i // 2 + direction) % ring) * 2 + i % 2))
    near = lax.ppermute(own, axis, step)
    far = lax.ppermute(near, axis, step)
    other = lax.ppermute(near, axis, swap)
    sign = 1 - 2 * core
    owners = [chip, (chip - sign) % ring, (chip + 2) % ring, (chip + sign) % ring]
    return [own, near, far, other], owners


def layer_norm(values, gain, shift):
    values = values.astype(jnp.float32)
    centre = values - jnp.mean(values, axis=-1, keepdims=True)
    spread = jnp.mean(centre * centre, axis=-1, keepdims=True)
    return centre * lax.rsqrt(spread + 1e-05) * gain + shift


def rms_norm(values, gain):
    values = values.astype(jnp.float32)
    return values * lax.rsqrt(jnp.mean(values * values, axis=-1, keepdims=True) + 1e-06) * gain


def masked_softmax(scores, valid):
    highest = jnp.max(jnp.where(valid, scores, -jnp.inf), axis=-1, keepdims=True)
    raised = jnp.where(valid, jnp.exp(scores - highest), jnp.zeros_like(scores))
    return (raised / jnp.sum(raised, axis=-1, keepdims=True)).astype(jnp.bfloat16)


def shards(
    audio,
    ln_gain,
    ln_shift,
    enc_wq,
    enc_bq,
    enc_wk,
    enc_wv,
    enc_bv,
    enc_wo,
    enc_bo,
    windows,
    dec_wkv,
    dec_bv,
    text,
    norm_gain,
    dec_wq,
    dec_bq,
    dec_wo,
    span_start,
    span_len,
):
    seq_count = lax.axis_size("seq")
    head_count = lax.axis_size("heads")
    seq_index = lax.axis_index("seq")
    head_index = lax.axis_index("heads")
    frames_dev = audio.shape[0]
    enc_width = audio.shape[1]
    heads_dev = windows.shape[0]
    head_size = enc_wq.shape[1] // heads_dev
    all_frames = frames_dev * seq_count
    hidden = layer_norm(audio, ln_gain, ln_shift).astype(jnp.bfloat16)
    enc_query = (jnp.dot(hidden, enc_wq, preferred_element_type=jnp.float32) + enc_bq).astype(
        jnp.bfloat16
    )
    enc_keys = jnp.dot(hidden, enc_wk, preferred_element_type=jnp.float32).astype(jnp.bfloat16)
    enc_values = (jnp.dot(hidden, enc_wv, preferred_element_type=jnp.float32) + enc_bv).astype(
        jnp.bfloat16
    )
    enc_pairs = jnp.stack([enc_keys, enc_values], axis=1)
    widened = with_halo(enc_pairs, (("seq", 0),), EWIN)
    extent = frames_dev + 2 * EWIN
    key_block = widened[:, 0, :].reshape(extent, heads_dev, head_size)
    value_block = widened[:, 1, :].reshape(extent, heads_dev, head_size)
    query_block = enc_query.reshape(frames_dev, heads_dev, head_size)
    scores = jnp.einsum(
        "qhd,khd->hqk", query_block, key_block, preferred_element_type=jnp.float32
    ) * head_size ** (-0.5)
    row_frames = seq_index * frames_dev + jnp.arange(frames_dev, dtype=jnp.int32)
    col_frames = seq_index * frames_dev - EWIN + jnp.arange(extent, dtype=jnp.int32)
    distance = jnp.abs(row_frames[:, None] - col_frames[None, :])
    inside = (col_frames >= 0) & (col_frames < all_frames)
    valid = (distance[None, :, :] <= windows[:, None, None]) & inside[None, None, :]
    enc_weights = masked_softmax(scores, valid)
    enc_context = jnp.einsum(
        "hqk,khd->qhd", enc_weights, value_block, preferred_element_type=jnp.float32
    )
    enc_context = enc_context.astype(jnp.bfloat16).reshape(frames_dev, heads_dev * head_size)
    share = frames_dev // head_count
    enc_term = jnp.dot(enc_context, enc_wo, preferred_element_type=jnp.float32)
    mixed = jnp.sum(
        lax.all_to_all(
            enc_term.reshape(head_count, share, enc_width), "heads", 0, 0, tiled=True
        ),
        axis=0,
    )
    own_audio = lax.dynamic_slice_in_dim(audio, head_index * share, share, 0)
    enc_out = (own_audio.astype(jnp.float32) + mixed + enc_bo).astype(jnp.bfloat16)
    groups = dec_wkv.shape[1]
    groups_dev = groups // head_count
    pair_width = dec_wkv.shape[2]
    dec_head = pair_width // 2
    band_bias = jnp.concatenate([jnp.zeros_like(dec_bv), dec_bv], axis=1)
    share_pairs = (
        jnp.dot(
            enc_out,
            dec_wkv.reshape(enc_width, groups * pair_width),
            preferred_element_type=jnp.float32,
        )
        + band_bias.reshape(groups * pair_width)
    ).astype(jnp.bfloat16)
    band_pairs = lax.all_to_all(share_pairs, "heads", 1, 0, tiled=True)
    band_pairs = band_pairs.reshape(frames_dev, groups_dev, pair_width)
    band_wide = with_halo(band_pairs, (("seq", 0),), BAND)
    rows_dev = text.shape[0]
    model_width = text.shape[1]
    query_width = dec_wq.shape[1]
    query_heads = query_width // (groups_dev * dec_head)
    normed = rms_norm(text, norm_gain).astype(jnp.bfloat16)
    query_sum = jnp.dot(
        normed,
        lax.all_gather(dec_wq, "seq", axis=0, tiled=True),
        preferred_element_type=jnp.float32,
    )
    dec_query = (
        (query_sum + dec_bq)
        .astype(jnp.bfloat16)
        .reshape(rows_dev, groups_dev, query_heads, dec_head)
    )
    band_extent = band_wide.shape[0]
    band_keys = band_wide[:, :, :dec_head]
    band_values = band_wide[:, :, dec_head:]
    dec_scores = jnp.einsum(
        "rgqd,kgd->rgqk", dec_query, band_keys, preferred_element_type=jnp.float32
    ) * dec_head ** (-0.5)
    band_frames = seq_index * frames_dev - BAND + jnp.arange(band_extent, dtype=jnp.int32)
    in_band = (band_frames[None, :] >= span_start[:, None]) & (
        band_frames[None, :] < (span_start + span_len)[:, None]
    )
    dec_weights = masked_softmax(dec_scores, in_band[:, None, None, :])
    dec_context = jnp.einsum(
        "rgqk,kgd->rgqd", dec_weights, band_values, preferred_element_type=jnp.float32
    )
    dec_context = dec_context.astype(jnp.bfloat16).reshape(rows_dev, query_width)
    ratio = seq_count // head_count
    set_rows = dec_wo.shape[0]
    block_cols = dec_wo.shape[1]
    flat = [(c, j) for c in range(seq_count) for j in range(head_count)]
    regroup = [
        (c * head_count + j, (ratio * j + c % ratio) * head_count + c // ratio) for c, j in flat
    ]
    piece = lax.ppermute(dec_wo, ("seq", "heads"), regroup)
    pieces, owners = heads_ring_gather(dec_context, "heads")
    set_cols = ratio * block_cols
    column_weight = lax.all_gather(piece, "seq", axis=1, tiled=True)
    total = jnp.zeros((rows_dev, set_cols), jnp.float32)
    for held, owner in zip(pieces, owners):
        for offset in range(held.shape[0]):
            weight_set = lax.dynamic_slice_in_dim(
                column_weight, (owner * held.shape[0] + offset) * set_cols, set_cols, 1
            )
            term = jnp.dot(held[offset], weight_set, preferred_element_type=jnp.float32)
            total = total + term.astype(jnp.bfloat16).astype(jnp.float32)
    summed = total
    col_share = model_width // head_count
    own_text = lax.dynamic_slice_in_dim(text, head_index * col_share, col_share, 1)
    dec_out = (own_text.astype(jnp.float32) + summed).astype(jnp.bfloat16)
    return (enc_out, dec_out)


def solution(mesh):
    return jax.shard_map(
        shards,
        mesh=mesh,
        in_specs=(
            P("seq", None),
            P(),
            P(),
            P(None, "heads"),
            P("heads"),
            P(None, "heads"),
            P(None, "heads"),
            P("heads"),
            P("heads", None),
            P(),
            P("heads"),
            P(),
            P(),
            P("seq", None),
            P(),
            P("seq", "heads"),
            P("heads"),
            P("heads", "seq"),
            P("seq"),
            P("seq"),
        ),
        out_specs=(P(("seq", "heads"), None), P("seq", "heads")),
        check_vma=False,
    )
```

```python
import jax
import jax.numpy as jnp
from jax import lax
from jax.sharding import PartitionSpec as P

EWIN = 128
BAND = 256
SEQ_OUTER = 4


def with_halo(block, sides, width):
    for axis, dim in sides:
        count = lax.axis_size(axis)
        forward = [(i, i + 1) for i in range(count - 1)]
        backward = [(target, source) for source, target in forward]
        low = lax.ppermute(
            lax.slice_in_dim(block, block.shape[dim] - width, None, axis=dim), axis, forward
        )
        high = lax.ppermute(lax.slice_in_dim(block, 0, width, axis=dim), axis, backward)
        block = jnp.concatenate([low, block, high], axis=dim)
    return block


def ring_gather(piece, axis, stride, count, split_dim):
    size = lax.axis_size(axis)

    def shifted(step):
        pairs = []
        for source in range(size):
            ring_pos = (source // stride) % count
            base = source - ring_pos * stride
            pairs.append((source, base + ((ring_pos + step) % count) * stride))
        return pairs

    from_behind = lax.ppermute(piece, axis, shifted(1))
    from_ahead = lax.ppermute(piece, axis, shifted(-1))
    half = piece.shape[split_dim] // 2
    first = lax.ppermute(lax.slice_in_dim(from_behind, 0, half, axis=split_dim), axis, shifted(1))
    second = lax.ppermute(lax.slice_in_dim(from_ahead, half, None, axis=split_dim), axis, shifted(-1))
    opposite = jnp.concatenate([first, second], axis=split_dim)
    return [piece, from_ahead, opposite, from_behind]


def heads_ring_gather(block, axis):
    count = lax.axis_size(axis)
    ring = count // 2
    index = lax.axis_index(axis)
    chip = index // 2
    core = index % 2
    swap = [(i, i ^ 1) for i in range(count)]
    sibling = lax.ppermute(block, axis, swap)
    own = jnp.where(core == 0, jnp.stack([block, sibling]), jnp.stack([sibling, block]))
    step = []
    for i in range(count):
        direction = 1 if i % 2 == 0 else -1
        step.append((i, ((i // 2 + direction) % ring) * 2 + i % 2))
    near = lax.ppermute(own, axis, step)
    far = lax.ppermute(near, axis, step)
    other = lax.ppermute(near, axis, swap)
    sign = 1 - 2 * core
    owners = [chip, (chip - sign) % ring, (chip + 2) % ring, (chip + sign) % ring]
    return [own, near, far, other], owners


def layer_norm(values, gain, shift):
    values = values.astype(jnp.float32)
    centre = values - jnp.mean(values, axis=-1, keepdims=True)
    spread = jnp.mean(centre * centre, axis=-1, keepdims=True)
    return centre * lax.rsqrt(spread + 1e-05) * gain + shift


def rms_norm(values, gain):
    values = values.astype(jnp.float32)
    return values * lax.rsqrt(jnp.mean(values * values, axis=-1, keepdims=True) + 1e-06) * gain


def masked_softmax(scores, valid):
    highest = jnp.max(jnp.where(valid, scores, -jnp.inf), axis=-1, keepdims=True)
    raised = jnp.where(valid, jnp.exp(scores - highest), jnp.zeros_like(scores))
    return (raised / jnp.sum(raised, axis=-1, keepdims=True)).astype(jnp.bfloat16)


def layer_body(
    audio,
    ln_gain,
    ln_shift,
    enc_wq,
    enc_bq,
    enc_wk,
    enc_wv,
    enc_bv,
    enc_wo,
    enc_bo,
    windows,
    dec_wkv,
    dec_bv,
    text,
    norm_gain,
    dec_wq,
    dec_bq,
    dec_wo,
    span_start,
    span_len,
):
    seq_count = lax.axis_size("seq")
    head_count = lax.axis_size("heads")
    seq_index = lax.axis_index("seq")
    head_index = lax.axis_index("heads")
    frames_dev = audio.shape[0]
    enc_width = audio.shape[1]
    heads_dev = windows.shape[0]
    head_size = enc_wq.shape[1] // heads_dev
    all_frames = frames_dev * seq_count
    ratio = seq_count // head_count
    block_cols = dec_wo.shape[1]
    flat = [(c, j) for c in range(seq_count) for j in range(head_count)]
    regroup = [
        (c * head_count + j, (ratio * j + c % ratio) * head_count + c // ratio) for c, j in flat
    ]
    piece = lax.ppermute(dec_wo, ("seq", "heads"), regroup)
    column_weight = lax.all_gather(piece, "seq", axis=1, tiled=True)
    hidden = layer_norm(audio, ln_gain, ln_shift).astype(jnp.bfloat16)
    enc_query = (jnp.dot(hidden, enc_wq, preferred_element_type=jnp.float32) + enc_bq).astype(
        jnp.bfloat16
    )
    enc_keys = jnp.dot(hidden, enc_wk, preferred_element_type=jnp.float32).astype(jnp.bfloat16)
    enc_values = (jnp.dot(hidden, enc_wv, preferred_element_type=jnp.float32) + enc_bv).astype(
        jnp.bfloat16
    )
    enc_pairs = jnp.stack([enc_keys, enc_values], axis=1)
    widened = with_halo(enc_pairs, (("seq", 0),), EWIN)
    extent = frames_dev + 2 * EWIN
    key_block = widened[:, 0, :].reshape(extent, heads_dev, head_size)
    value_block = widened[:, 1, :].reshape(extent, heads_dev, head_size)
    query_block = enc_query.reshape(frames_dev, heads_dev, head_size)
    scores = jnp.einsum(
        "qhd,khd->hqk", query_block, key_block, preferred_element_type=jnp.float32
    ) * head_size ** (-0.5)
    row_frames = seq_index * frames_dev + jnp.arange(frames_dev, dtype=jnp.int32)
    col_frames = seq_index * frames_dev - EWIN + jnp.arange(extent, dtype=jnp.int32)
    distance = jnp.abs(row_frames[:, None] - col_frames[None, :])
    inside = (col_frames >= 0) & (col_frames < all_frames)
    valid = (distance[None, :, :] <= windows[:, None, None]) & inside[None, None, :]
    enc_weights = masked_softmax(scores, valid)
    enc_context = jnp.einsum(
        "hqk,khd->qhd", enc_weights, value_block, preferred_element_type=jnp.float32
    )
    enc_context = enc_context.astype(jnp.bfloat16).reshape(frames_dev, heads_dev * head_size)
    share = frames_dev // head_count
    enc_term = jnp.dot(enc_context, enc_wo, preferred_element_type=jnp.float32)
    mixed = jnp.sum(
        lax.all_to_all(
            enc_term.reshape(head_count, share, enc_width), "heads", 0, 0, tiled=True
        ),
        axis=0,
    )
    own_audio = lax.dynamic_slice_in_dim(audio, head_index * share, share, 0)
    enc_out = (own_audio.astype(jnp.float32) + mixed + enc_bo).astype(jnp.bfloat16)
    groups = dec_wkv.shape[1]
    groups_dev = groups // head_count
    pair_width = dec_wkv.shape[2]
    dec_head = pair_width // 2
    band_bias = jnp.concatenate([jnp.zeros_like(dec_bv), dec_bv], axis=1)
    share_pairs = (
        jnp.dot(
            enc_out,
            dec_wkv.reshape(enc_width, groups * pair_width),
            preferred_element_type=jnp.float32,
        )
        + band_bias.reshape(groups * pair_width)
    ).astype(jnp.bfloat16)
    band_pairs = lax.all_to_all(share_pairs, "heads", 1, 0, tiled=True)
    band_pairs = band_pairs.reshape(frames_dev, groups_dev, pair_width)
    band_wide = with_halo(band_pairs, (("seq", 0),), BAND)
    rows_dev = text.shape[0]
    model_width = text.shape[1]
    query_width = dec_wq.shape[1]
    query_heads = query_width // (groups_dev * dec_head)
    normed = rms_norm(text, norm_gain).astype(jnp.bfloat16)
    ring = SEQ_OUTER
    outer = seq_index // ring
    inner = seq_index % ring
    k_rows = dec_wq.shape[0]
    half_rows = k_rows // 2
    by_inner = jnp.stack(ring_gather(dec_wq[:half_rows], "seq", 1, ring, 1))
    first_half = ring_gather(by_inner, "seq", ring, ring, 2)
    by_outer = jnp.stack(ring_gather(dec_wq[half_rows:], "seq", ring, ring, 1))
    second_half = ring_gather(by_outer, "seq", 1, ring, 2)
    query_sum = jnp.zeros((rows_dev, query_width), jnp.float32)
    for step_outer in range(ring):
        for step_inner in range(ring):
            source = ((outer + step_outer) % ring) * ring + (inner + step_inner) % ring
            normed_block = lax.dynamic_slice_in_dim(normed, source * k_rows, k_rows, 1)
            query_sum = query_sum + jnp.dot(
                normed_block[:, :half_rows],
                first_half[step_outer][step_inner],
                preferred_element_type=jnp.float32,
            )
            query_sum = query_sum + jnp.dot(
                normed_block[:, half_rows:],
                second_half[step_inner][step_outer],
                preferred_element_type=jnp.float32,
            )
    dec_query = (
        (query_sum + dec_bq)
        .astype(jnp.bfloat16)
        .reshape(rows_dev, groups_dev, query_heads, dec_head)
    )
    band_extent = band_wide.shape[0]
    band_keys = band_wide[:, :, :dec_head]
    band_values = band_wide[:, :, dec_head:]
    dec_scores = jnp.einsum(
        "rgqd,kgd->rgqk", dec_query, band_keys, preferred_element_type=jnp.float32
    ) * dec_head ** (-0.5)
    band_frames = seq_index * frames_dev - BAND + jnp.arange(band_extent, dtype=jnp.int32)
    in_band = (band_frames[None, :] >= span_start[:, None]) & (
        band_frames[None, :] < (span_start + span_len)[:, None]
    )
    dec_weights = masked_softmax(dec_scores, in_band[:, None, None, :])
    dec_context = jnp.einsum(
        "rgqk,kgd->rgqd", dec_weights, band_values, preferred_element_type=jnp.float32
    )
    dec_context = dec_context.astype(jnp.bfloat16).reshape(rows_dev, query_width)
    pieces, owners = heads_ring_gather(dec_context, "heads")
    set_cols = ratio * block_cols
    total = jnp.zeros((rows_dev, set_cols), jnp.float32)
    for held, owner in zip(pieces, owners):
        for offset in range(held.shape[0]):
            weight_set = lax.dynamic_slice_in_dim(
                column_weight, (owner * held.shape[0] + offset) * set_cols, set_cols, 1
            )
            term = jnp.dot(held[offset], weight_set, preferred_element_type=jnp.float32)
            total = total + term.astype(jnp.bfloat16).astype(jnp.float32)
    summed = total
    col_share = model_width // head_count
    own_text = lax.dynamic_slice_in_dim(text, head_index * col_share, col_share, 1)
    dec_out = (own_text.astype(jnp.float32) + summed).astype(jnp.bfloat16)
    return (enc_out, dec_out)


def solution(mesh):
    return jax.shard_map(
        layer_body,
        mesh=mesh,
        in_specs=(
            P("seq", None),
            P(),
            P(),
            P(None, "heads"),
            P("heads"),
            P(None, "heads"),
            P(None, "heads"),
            P("heads"),
            P("heads", None),
            P(),
            P("heads"),
            P(),
            P(),
            P("seq", None),
            P(),
            P("seq", "heads"),
            P("heads"),
            P("heads", "seq"),
            P("seq"),
            P("seq"),
        ),
        out_specs=(P(("seq", "heads"), None), P("seq", "heads")),
        check_vma=False,
    )
```

```python
import jax
import jax.numpy as jnp
from jax import lax
from jax.sharding import PartitionSpec as P

EWIN = 128
BAND = 256


def with_halo(block, sides, width):
    for axis, dim in sides:
        count = lax.axis_size(axis)
        forward = [(i, i + 1) for i in range(count - 1)]
        backward = [(target, source) for source, target in forward]
        low = lax.ppermute(
            lax.slice_in_dim(block, block.shape[dim] - width, None, axis=dim), axis, forward
        )
        high = lax.ppermute(lax.slice_in_dim(block, 0, width, axis=dim), axis, backward)
        block = jnp.concatenate([low, block, high], axis=dim)
    return block


def heads_gather(block, axis):
    count = lax.axis_size(axis)
    index = lax.axis_index(axis)
    gathered = block[None]
    bit = 1
    while bit < count:
        other = lax.ppermute(gathered, axis, [(i, i ^ bit) for i in range(count)])
        upper = (index & bit) != 0
        gathered = jnp.where(
            upper,
            jnp.concatenate([other, gathered], axis=0),
            jnp.concatenate([gathered, other], axis=0),
        )
        bit *= 2
    return gathered


def heads_ring_gather(block, axis):
    count = lax.axis_size(axis)
    ring = count // 2
    index = lax.axis_index(axis)
    chip = index // 2
    core = index % 2
    swap = [(i, i ^ 1) for i in range(count)]
    sibling = lax.ppermute(block, axis, swap)
    own = jnp.where(core == 0, jnp.stack([block, sibling]), jnp.stack([sibling, block]))
    step = []
    for i in range(count):
        direction = 1 if i % 2 == 0 else -1
        step.append((i, ((i // 2 + direction) % ring) * 2 + i % 2))
    near = lax.ppermute(own, axis, step)
    far = lax.ppermute(near, axis, step)
    other = lax.ppermute(near, axis, swap)
    sign = 1 - 2 * core
    owners = [chip, (chip - sign) % ring, (chip + 2) % ring, (chip + sign) % ring]
    return [own, near, far, other], owners


def layer_norm(values, gain, shift):
    values = values.astype(jnp.float32)
    centre = values - jnp.mean(values, axis=-1, keepdims=True)
    spread = jnp.mean(centre * centre, axis=-1, keepdims=True)
    return centre * lax.rsqrt(spread + 1e-05) * gain + shift


def rms_norm(values, gain):
    values = values.astype(jnp.float32)
    return values * lax.rsqrt(jnp.mean(values * values, axis=-1, keepdims=True) + 1e-06) * gain


def masked_softmax(scores, valid):
    highest = jnp.max(jnp.where(valid, scores, -jnp.inf), axis=-1, keepdims=True)
    raised = jnp.where(valid, jnp.exp(scores - highest), jnp.zeros_like(scores))
    return (raised / jnp.sum(raised, axis=-1, keepdims=True)).astype(jnp.bfloat16)


def shards(
    audio,
    ln_gain,
    ln_shift,
    enc_wq,
    enc_bq,
    enc_wk,
    enc_wv,
    enc_bv,
    enc_wo,
    enc_bo,
    windows,
    dec_wkv,
    dec_bv,
    text,
    norm_gain,
    dec_wq,
    dec_bq,
    dec_wo,
    span_start,
    span_len,
):
    seq_count = lax.axis_size("seq")
    head_count = lax.axis_size("heads")
    seq_index = lax.axis_index("seq")
    head_index = lax.axis_index("heads")
    frames_dev = audio.shape[0]
    enc_width = audio.shape[1]
    heads_dev = windows.shape[0]
    head_size = enc_wq.shape[1] // heads_dev
    all_frames = frames_dev * seq_count
    hidden = layer_norm(audio, ln_gain, ln_shift).astype(jnp.bfloat16)
    enc_query = (jnp.dot(hidden, enc_wq, preferred_element_type=jnp.float32) + enc_bq).astype(
        jnp.bfloat16
    )
    enc_keys = jnp.dot(hidden, enc_wk, preferred_element_type=jnp.float32).astype(jnp.bfloat16)
    enc_values = (jnp.dot(hidden, enc_wv, preferred_element_type=jnp.float32) + enc_bv).astype(
        jnp.bfloat16
    )
    enc_pairs = jnp.stack([enc_keys, enc_values], axis=1)
    widened = with_halo(enc_pairs, (("seq", 0),), EWIN)
    extent = frames_dev + 2 * EWIN
    key_block = widened[:, 0, :].reshape(extent, heads_dev, head_size)
    value_block = widened[:, 1, :].reshape(extent, heads_dev, head_size)
    query_block = enc_query.reshape(frames_dev, heads_dev, head_size)
    scores = jnp.einsum(
        "qhd,khd->hqk", query_block, key_block, preferred_element_type=jnp.float32
    ) * head_size ** (-0.5)
    row_frames = seq_index * frames_dev + jnp.arange(frames_dev, dtype=jnp.int32)
    col_frames = seq_index * frames_dev - EWIN + jnp.arange(extent, dtype=jnp.int32)
    distance = jnp.abs(row_frames[:, None] - col_frames[None, :])
    inside = (col_frames >= 0) & (col_frames < all_frames)
    valid = (distance[None, :, :] <= windows[:, None, None]) & inside[None, None, :]
    enc_weights = masked_softmax(scores, valid)
    enc_context = jnp.einsum(
        "hqk,khd->qhd", enc_weights, value_block, preferred_element_type=jnp.float32
    )
    enc_context = enc_context.astype(jnp.bfloat16).reshape(frames_dev, heads_dev * head_size)
    share = frames_dev // head_count
    enc_term = jnp.dot(enc_context, enc_wo, preferred_element_type=jnp.float32)
    mixed = jnp.sum(
        lax.all_to_all(
            enc_term.astype(jnp.bfloat16).reshape(head_count, share, enc_width),
            "heads",
            0,
            0,
            tiled=True,
        ).astype(jnp.float32),
        axis=0,
    )
    own_audio = lax.dynamic_slice_in_dim(audio, head_index * share, share, 0)
    enc_out = (own_audio.astype(jnp.float32) + mixed + enc_bo).astype(jnp.bfloat16)
    groups = dec_wkv.shape[1]
    groups_dev = groups // head_count
    pair_width = dec_wkv.shape[2]
    dec_head = pair_width // 2
    band_bias = jnp.concatenate([jnp.zeros_like(dec_bv), dec_bv], axis=1)
    share_pairs = (
        jnp.dot(
            enc_out,
            dec_wkv.reshape(enc_width, groups * pair_width),
            preferred_element_type=jnp.float32,
        )
        + band_bias.reshape(groups * pair_width)
    ).astype(jnp.bfloat16)
    band_pairs = lax.all_to_all(share_pairs, "heads", 1, 0, tiled=True)
    band_pairs = band_pairs.reshape(frames_dev, groups_dev, pair_width)
    band_wide = with_halo(band_pairs, (("seq", 0),), BAND)
    rows_dev = text.shape[0]
    model_width = text.shape[1]
    query_width = dec_wq.shape[1]
    query_heads = query_width // (groups_dev * dec_head)
    normed = rms_norm(text, norm_gain).astype(jnp.bfloat16)
    query_sum = jnp.dot(
        normed,
        lax.all_gather(dec_wq, "seq", axis=0, tiled=True),
        preferred_element_type=jnp.float32,
    )
    dec_query = (
        (query_sum + dec_bq)
        .astype(jnp.bfloat16)
        .reshape(rows_dev, groups_dev, query_heads, dec_head)
    )
    band_extent = band_wide.shape[0]
    band_keys = band_wide[:, :, :dec_head]
    band_values = band_wide[:, :, dec_head:]
    dec_scores = jnp.einsum(
        "rgqd,kgd->rgqk", dec_query, band_keys, preferred_element_type=jnp.float32
    ) * dec_head ** (-0.5)
    band_frames = seq_index * frames_dev - BAND + jnp.arange(band_extent, dtype=jnp.int32)
    in_band = (band_frames[None, :] >= span_start[:, None]) & (
        band_frames[None, :] < (span_start + span_len)[:, None]
    )
    dec_weights = masked_softmax(dec_scores, in_band[:, None, None, :])
    dec_context = jnp.einsum(
        "rgqk,kgd->rgqd", dec_weights, band_values, preferred_element_type=jnp.float32
    )
    dec_context = dec_context.astype(jnp.bfloat16).reshape(rows_dev, query_width)
    ratio = seq_count // head_count
    set_rows = dec_wo.shape[0]
    block_cols = dec_wo.shape[1]
    flat = [(c, j) for c in range(seq_count) for j in range(head_count)]
    regroup = [
        (c * head_count + j, (ratio * j + c % ratio) * head_count + c // ratio) for c, j in flat
    ]
    piece = lax.ppermute(dec_wo, ("seq", "heads"), regroup)
    pieces, owners = heads_ring_gather(dec_context, "heads")
    set_cols = ratio * block_cols
    column_weight = lax.all_gather(piece, "seq", axis=1, tiled=True)
    total = jnp.zeros((rows_dev, set_cols), jnp.float32)
    for held, owner in zip(pieces, owners):
        for offset in range(held.shape[0]):
            weight_set = lax.dynamic_slice_in_dim(
                column_weight, (owner * held.shape[0] + offset) * set_cols, set_cols, 1
            )
            term = jnp.dot(held[offset], weight_set, preferred_element_type=jnp.float32)
            total = total + term.astype(jnp.bfloat16).astype(jnp.float32)
    summed = total
    col_share = model_width // head_count
    own_text = lax.dynamic_slice_in_dim(text, head_index * col_share, col_share, 1)
    dec_out = (own_text.astype(jnp.float32) + summed).astype(jnp.bfloat16)
    return (enc_out, dec_out)


def solution(mesh):
    return jax.shard_map(
        shards,
        mesh=mesh,
        in_specs=(
            P("seq", None),
            P(),
            P(),
            P(None, "heads"),
            P("heads"),
            P(None, "heads"),
            P(None, "heads"),
            P("heads"),
            P("heads", None),
            P(),
            P("heads"),
            P(),
            P(),
            P("seq", None),
            P(),
            P("seq", "heads"),
            P("heads"),
            P("heads", "seq"),
            P("seq"),
            P("seq"),
        ),
        out_specs=(P(("seq", "heads"), None), P("seq", "heads")),
        check_vma=False,
    )
```

```python
import jax
import jax.numpy as jnp
from jax import lax
from jax.sharding import PartitionSpec as P

EWIN = 128
BAND = 256


def with_halo(block, sides, width):
    for axis, dim in sides:
        count = lax.axis_size(axis)
        forward = [(i, i + 1) for i in range(count - 1)]
        backward = [(target, source) for source, target in forward]
        low = lax.ppermute(
            lax.slice_in_dim(block, block.shape[dim] - width, None, axis=dim), axis, forward
        )
        high = lax.ppermute(lax.slice_in_dim(block, 0, width, axis=dim), axis, backward)
        block = jnp.concatenate([low, block, high], axis=dim)
    return block


def heads_gather(block, axis):
    count = lax.axis_size(axis)
    index = lax.axis_index(axis)
    gathered = block[None]
    bit = 1
    while bit < count:
        other = lax.ppermute(gathered, axis, [(i, i ^ bit) for i in range(count)])
        upper = (index & bit) != 0
        gathered = jnp.where(
            upper,
            jnp.concatenate([other, gathered], axis=0),
            jnp.concatenate([gathered, other], axis=0),
        )
        bit *= 2
    return gathered


def heads_ring_gather(block, axis):
    count = lax.axis_size(axis)
    ring = count // 2
    index = lax.axis_index(axis)
    chip = index // 2
    core = index % 2
    swap = [(i, i ^ 1) for i in range(count)]
    sibling = lax.ppermute(block, axis, swap)
    own = jnp.where(core == 0, jnp.stack([block, sibling]), jnp.stack([sibling, block]))
    step = []
    for i in range(count):
        direction = 1 if i % 2 == 0 else -1
        step.append((i, ((i // 2 + direction) % ring) * 2 + i % 2))
    near = lax.ppermute(own, axis, step)
    far = lax.ppermute(near, axis, step)
    other = lax.ppermute(near, axis, swap)
    sign = 1 - 2 * core
    owners = [chip, (chip - sign) % ring, (chip + 2) % ring, (chip + sign) % ring]
    return [own, near, far, other], owners


def layer_norm(values, gain, shift):
    values = values.astype(jnp.float32)
    centre = values - jnp.mean(values, axis=-1, keepdims=True)
    spread = jnp.mean(centre * centre, axis=-1, keepdims=True)
    return centre * lax.rsqrt(spread + 1e-05) * gain + shift


def rms_norm(values, gain):
    values = values.astype(jnp.float32)
    return values * lax.rsqrt(jnp.mean(values * values, axis=-1, keepdims=True) + 1e-06) * gain


def masked_softmax(scores, valid):
    highest = jnp.max(jnp.where(valid, scores, -jnp.inf), axis=-1, keepdims=True)
    raised = jnp.where(valid, jnp.exp(scores - highest), jnp.zeros_like(scores))
    return (raised / jnp.sum(raised, axis=-1, keepdims=True)).astype(jnp.bfloat16)


def shards(
    audio,
    ln_gain,
    ln_shift,
    enc_wq,
    enc_bq,
    enc_wk,
    enc_wv,
    enc_bv,
    enc_wo,
    enc_bo,
    windows,
    dec_wkv,
    dec_bv,
    text,
    norm_gain,
    dec_wq,
    dec_bq,
    dec_wo,
    span_start,
    span_len,
):
    seq_count = lax.axis_size("seq")
    head_count = lax.axis_size("heads")
    seq_index = lax.axis_index("seq")
    head_index = lax.axis_index("heads")
    frames_dev = audio.shape[0]
    enc_width = audio.shape[1]
    heads_dev = windows.shape[0]
    head_size = enc_wq.shape[1] // heads_dev
    all_frames = frames_dev * seq_count
    hidden = layer_norm(audio, ln_gain, ln_shift).astype(jnp.bfloat16)
    enc_query = (jnp.dot(hidden, enc_wq, preferred_element_type=jnp.float32) + enc_bq).astype(
        jnp.bfloat16
    )
    enc_keys = jnp.dot(hidden, enc_wk, preferred_element_type=jnp.float32).astype(jnp.bfloat16)
    enc_values = (jnp.dot(hidden, enc_wv, preferred_element_type=jnp.float32) + enc_bv).astype(
        jnp.bfloat16
    )
    enc_pairs = jnp.stack([enc_keys, enc_values], axis=1)
    widened = with_halo(enc_pairs, (("seq", 0),), EWIN)
    extent = frames_dev + 2 * EWIN
    key_block = widened[:, 0, :].reshape(extent, heads_dev, head_size)
    value_block = widened[:, 1, :].reshape(extent, heads_dev, head_size)
    query_block = enc_query.reshape(frames_dev, heads_dev, head_size)
    scores = jnp.einsum(
        "qhd,khd->hqk", query_block, key_block, preferred_element_type=jnp.float32
    ) * head_size ** (-0.5)
    row_frames = seq_index * frames_dev + jnp.arange(frames_dev, dtype=jnp.int32)
    col_frames = seq_index * frames_dev - EWIN + jnp.arange(extent, dtype=jnp.int32)
    distance = jnp.abs(row_frames[:, None] - col_frames[None, :])
    inside = (col_frames >= 0) & (col_frames < all_frames)
    valid = (distance[None, :, :] <= windows[:, None, None]) & inside[None, None, :]
    enc_weights = masked_softmax(scores, valid)
    enc_context = jnp.einsum(
        "hqk,khd->qhd", enc_weights, value_block, preferred_element_type=jnp.float32
    )
    enc_context = enc_context.astype(jnp.bfloat16).reshape(frames_dev, heads_dev * head_size)
    share = frames_dev // head_count
    enc_term = jnp.dot(enc_context, enc_wo, preferred_element_type=jnp.float32)
    mixed = jnp.sum(
        lax.all_to_all(
            enc_term.astype(jnp.bfloat16).reshape(head_count, share, enc_width),
            "heads",
            0,
            0,
            tiled=True,
        ).astype(jnp.float32),
        axis=0,
    )
    own_audio = lax.dynamic_slice_in_dim(audio, head_index * share, share, 0)
    enc_out = (own_audio.astype(jnp.float32) + mixed + enc_bo).astype(jnp.bfloat16)
    groups = dec_wkv.shape[1]
    groups_dev = groups // head_count
    pair_width = dec_wkv.shape[2]
    dec_head = pair_width // 2
    band_bias = jnp.concatenate([jnp.zeros_like(dec_bv), dec_bv], axis=1)
    share_pairs = (
        jnp.dot(
            enc_out,
            dec_wkv.reshape(enc_width, groups * pair_width),
            preferred_element_type=jnp.float32,
        )
        + band_bias.reshape(groups * pair_width)
    ).astype(jnp.bfloat16)
    band_pairs = lax.all_to_all(share_pairs, "heads", 1, 0, tiled=True)
    band_pairs = band_pairs.reshape(frames_dev, groups_dev, pair_width)
    band_wide = with_halo(band_pairs, (("seq", 0),), BAND)
    rows_dev = text.shape[0]
    model_width = text.shape[1]
    query_width = dec_wq.shape[1]
    query_heads = query_width // (groups_dev * dec_head)
    normed = rms_norm(text, norm_gain).astype(jnp.bfloat16)
    query_sum = jnp.dot(
        normed,
        lax.all_gather(dec_wq, "seq", axis=0, tiled=True),
        preferred_element_type=jnp.float32,
    )
    dec_query = (
        (query_sum + dec_bq)
        .astype(jnp.bfloat16)
        .reshape(rows_dev, groups_dev, query_heads, dec_head)
    )
    band_extent = band_wide.shape[0]
    band_keys = band_wide[:, :, :dec_head]
    band_values = band_wide[:, :, dec_head:]
    dec_scores = jnp.einsum(
        "rgqd,kgd->rgqk", dec_query, band_keys, preferred_element_type=jnp.float32
    ) * dec_head ** (-0.5)
    band_frames = seq_index * frames_dev - BAND + jnp.arange(band_extent, dtype=jnp.int32)
    in_band = (band_frames[None, :] >= span_start[:, None]) & (
        band_frames[None, :] < (span_start + span_len)[:, None]
    )
    dec_weights = masked_softmax(dec_scores, in_band[:, None, None, :])
    dec_context = jnp.einsum(
        "rgqk,kgd->rgqd", dec_weights, band_values, preferred_element_type=jnp.float32
    )
    dec_context = dec_context.astype(jnp.bfloat16).reshape(rows_dev, query_width)
    ratio = seq_count // head_count
    set_rows = dec_wo.shape[0]
    block_cols = dec_wo.shape[1]
    flat = [(c, j) for c in range(seq_count) for j in range(head_count)]
    regroup = [
        (c * head_count + j, (ratio * j + c % ratio) * head_count + c // ratio) for c, j in flat
    ]
    held_wo, _ = lax.optimization_barrier((dec_wo, enc_out))
    piece = lax.ppermute(held_wo, ("seq", "heads"), regroup)
    pieces, owners = heads_ring_gather(dec_context, "heads")
    set_cols = ratio * block_cols
    column_weight = lax.all_gather(piece, "seq", axis=1, tiled=True)
    total = jnp.zeros((rows_dev, set_cols), jnp.float32)
    for held, owner in zip(pieces, owners):
        for offset in range(held.shape[0]):
            weight_set = lax.dynamic_slice_in_dim(
                column_weight, (owner * held.shape[0] + offset) * set_cols, set_cols, 1
            )
            term = jnp.dot(held[offset], weight_set, preferred_element_type=jnp.float32)
            total = total + term.astype(jnp.bfloat16).astype(jnp.float32)
    summed = total
    col_share = model_width // head_count
    own_text = lax.dynamic_slice_in_dim(text, head_index * col_share, col_share, 1)
    dec_out = (own_text.astype(jnp.float32) + summed).astype(jnp.bfloat16)
    return (enc_out, dec_out)


def solution(mesh):
    return jax.shard_map(
        shards,
        mesh=mesh,
        in_specs=(
            P("seq", None),
            P(),
            P(),
            P(None, "heads"),
            P("heads"),
            P(None, "heads"),
            P(None, "heads"),
            P("heads"),
            P("heads", None),
            P(),
            P("heads"),
            P(),
            P(),
            P("seq", None),
            P(),
            P("seq", "heads"),
            P("heads"),
            P("heads", "seq"),
            P("seq"),
            P("seq"),
        ),
        out_specs=(P(("seq", "heads"), None), P("seq", "heads")),
        check_vma=False,
    )
```

```python
import jax
import jax.numpy as jnp
from jax import lax
from jax.sharding import PartitionSpec as P

EWIN = 128
BAND = 256


def with_halo(block, sides, width):
    for axis, dim in sides:
        count = lax.axis_size(axis)
        forward = [(i, i + 1) for i in range(count - 1)]
        backward = [(target, source) for source, target in forward]
        low = lax.ppermute(
            lax.slice_in_dim(block, block.shape[dim] - width, None, axis=dim), axis, forward
        )
        high = lax.ppermute(lax.slice_in_dim(block, 0, width, axis=dim), axis, backward)
        block = jnp.concatenate([low, block, high], axis=dim)
    return block


def heads_ring_gather(block, axis):
    count = lax.axis_size(axis)
    ring = count // 2
    index = lax.axis_index(axis)
    chip = index // 2
    core = index % 2
    swap = [(i, i ^ 1) for i in range(count)]
    sibling = lax.ppermute(block, axis, swap)
    own = jnp.where(core == 0, jnp.stack([block, sibling]), jnp.stack([sibling, block]))
    step = []
    for i in range(count):
        direction = 1 if i % 2 == 0 else -1
        step.append((i, ((i // 2 + direction) % ring) * 2 + i % 2))
    near = lax.ppermute(own, axis, step)
    far = lax.ppermute(near, axis, step)
    other = lax.ppermute(near, axis, swap)
    sign = 1 - 2 * core
    owners = [chip, (chip - sign) % ring, (chip + 2) % ring, (chip + sign) % ring]
    return [own, near, far, other], owners


def layer_norm(values, gain, shift):
    values = values.astype(jnp.float32)
    centre = values - jnp.mean(values, axis=-1, keepdims=True)
    spread = jnp.mean(centre * centre, axis=-1, keepdims=True)
    return centre * lax.rsqrt(spread + 1e-05) * gain + shift


def rms_norm(values, gain):
    values = values.astype(jnp.float32)
    return values * lax.rsqrt(jnp.mean(values * values, axis=-1, keepdims=True) + 1e-06) * gain


def masked_softmax(scores, valid):
    highest = jnp.max(jnp.where(valid, scores, -jnp.inf), axis=-1, keepdims=True)
    raised = jnp.where(valid, jnp.exp(scores - highest), jnp.zeros_like(scores))
    return (raised / jnp.sum(raised, axis=-1, keepdims=True)).astype(jnp.bfloat16)


def layer_body(
    audio,
    ln_gain,
    ln_shift,
    enc_wq,
    enc_bq,
    enc_wk,
    enc_wv,
    enc_bv,
    enc_wo,
    enc_bo,
    windows,
    dec_wkv,
    dec_bv,
    text,
    norm_gain,
    dec_wq,
    dec_bq,
    dec_wo,
    span_start,
    span_len,
):
    seq_count = lax.axis_size("seq")
    head_count = lax.axis_size("heads")
    seq_index = lax.axis_index("seq")
    head_index = lax.axis_index("heads")
    frames_dev = audio.shape[0]
    enc_width = audio.shape[1]
    heads_dev = windows.shape[0]
    head_size = enc_wq.shape[1] // heads_dev
    all_frames = frames_dev * seq_count
    hidden = layer_norm(audio, ln_gain, ln_shift).astype(jnp.bfloat16)
    enc_query = (jnp.dot(hidden, enc_wq, preferred_element_type=jnp.float32) + enc_bq).astype(
        jnp.bfloat16
    )
    enc_keys = jnp.dot(hidden, enc_wk, preferred_element_type=jnp.float32).astype(jnp.bfloat16)
    enc_values = (jnp.dot(hidden, enc_wv, preferred_element_type=jnp.float32) + enc_bv).astype(
        jnp.bfloat16
    )
    enc_pairs = jnp.stack([enc_keys, enc_values], axis=1)
    widened = with_halo(enc_pairs, (("seq", 0),), EWIN)
    extent = frames_dev + 2 * EWIN
    key_block = widened[:, 0, :].reshape(extent, heads_dev, head_size)
    value_block = widened[:, 1, :].reshape(extent, heads_dev, head_size)
    query_block = enc_query.reshape(frames_dev, heads_dev, head_size)
    scores = jnp.einsum(
        "qhd,khd->hqk", query_block, key_block, preferred_element_type=jnp.float32
    ) * head_size ** (-0.5)
    row_frames = seq_index * frames_dev + jnp.arange(frames_dev, dtype=jnp.int32)
    col_frames = seq_index * frames_dev - EWIN + jnp.arange(extent, dtype=jnp.int32)
    distance = jnp.abs(row_frames[:, None] - col_frames[None, :])
    inside = (col_frames >= 0) & (col_frames < all_frames)
    valid = (distance[None, :, :] <= windows[:, None, None]) & inside[None, None, :]
    enc_weights = masked_softmax(scores, valid)
    enc_context = jnp.einsum(
        "hqk,khd->qhd", enc_weights, value_block, preferred_element_type=jnp.float32
    )
    enc_context = enc_context.astype(jnp.bfloat16).reshape(frames_dev, heads_dev * head_size)
    share = frames_dev // head_count
    enc_term = jnp.dot(enc_context, enc_wo, preferred_element_type=jnp.float32)
    mixed = jnp.sum(
        lax.all_to_all(
            enc_term.astype(jnp.bfloat16).reshape(head_count, share, enc_width),
            "heads",
            0,
            0,
            tiled=True,
        ).astype(jnp.float32),
        axis=0,
    )
    own_audio = lax.dynamic_slice_in_dim(audio, head_index * share, share, 0)
    enc_out = (own_audio.astype(jnp.float32) + mixed + enc_bo).astype(jnp.bfloat16)
    groups = dec_wkv.shape[1]
    groups_dev = groups // head_count
    pair_width = dec_wkv.shape[2]
    dec_head = pair_width // 2
    band_bias = jnp.concatenate([jnp.zeros_like(dec_bv), dec_bv], axis=1)
    share_pairs = (
        jnp.dot(
            enc_out,
            dec_wkv.reshape(enc_width, groups * pair_width),
            preferred_element_type=jnp.float32,
        )
        + band_bias.reshape(groups * pair_width)
    ).astype(jnp.bfloat16)
    band_pairs = lax.all_to_all(share_pairs, "heads", 1, 0, tiled=True)
    band_pairs = band_pairs.reshape(frames_dev, groups_dev, pair_width)
    band_wide = with_halo(band_pairs, (("seq", 0),), BAND)
    rows_dev = text.shape[0]
    model_width = text.shape[1]
    query_width = dec_wq.shape[1]
    query_heads = query_width // (groups_dev * dec_head)
    normed = rms_norm(text, norm_gain).astype(jnp.bfloat16)
    query_sum = jnp.dot(
        normed,
        lax.all_gather(dec_wq, "seq", axis=0, tiled=True),
        preferred_element_type=jnp.float32,
    )
    dec_query = (
        (query_sum + dec_bq)
        .astype(jnp.bfloat16)
        .reshape(rows_dev, groups_dev, query_heads, dec_head)
    )
    band_extent = band_wide.shape[0]
    band_keys = band_wide[:, :, :dec_head]
    band_values = band_wide[:, :, dec_head:]
    dec_scores = jnp.einsum(
        "rgqd,kgd->rgqk", dec_query, band_keys, preferred_element_type=jnp.float32
    ) * dec_head ** (-0.5)
    band_frames = seq_index * frames_dev - BAND + jnp.arange(band_extent, dtype=jnp.int32)
    in_band = (band_frames[None, :] >= span_start[:, None]) & (
        band_frames[None, :] < (span_start + span_len)[:, None]
    )
    dec_weights = masked_softmax(dec_scores, in_band[:, None, None, :])
    dec_context = jnp.einsum(
        "rgqk,kgd->rgqd", dec_weights, band_values, preferred_element_type=jnp.float32
    )
    dec_context = dec_context.astype(jnp.bfloat16).reshape(rows_dev, query_width)
    ratio = seq_count // head_count
    set_rows = dec_wo.shape[0]
    block_cols = dec_wo.shape[1]
    flat = [(c, j) for c in range(seq_count) for j in range(head_count)]
    half_k = set_rows // ratio
    regroup_same = [
        (c * head_count + j, (ratio * j + c % ratio) * head_count + c // ratio) for c, j in flat
    ]
    regroup_other = [
        (c * head_count + j, (ratio * j + 1 - c % ratio) * head_count + c // ratio)
        for c, j in flat
    ]
    own_parity = lax.axis_index("seq") % ratio
    block_parity = lax.axis_index("seq") % ratio
    same_rows = lax.dynamic_slice_in_dim(dec_wo, block_parity * half_k, half_k, 0)
    other_rows = lax.dynamic_slice_in_dim(dec_wo, (1 - block_parity) * half_k, half_k, 0)
    same_piece = lax.ppermute(same_rows, ("seq", "heads"), regroup_same)
    other_piece = lax.ppermute(other_rows, ("seq", "heads"), regroup_other)
    first_piece = jnp.where(own_parity == 0, same_piece, other_piece)
    second_piece = jnp.where(own_parity == 0, other_piece, same_piece)
    first_weight = lax.all_gather(first_piece, "seq", axis=0, tiled=True)
    second_weight = lax.all_gather(second_piece, "seq", axis=0, tiled=True)
    pieces, owners = heads_ring_gather(dec_context, "heads")
    outputs = []
    for column_weight in (first_weight, second_weight):
        total = jnp.zeros((rows_dev, block_cols), jnp.float32)
        for held, owner in zip(pieces, owners):
            for offset in range(held.shape[0]):
                weight_set = lax.dynamic_slice_in_dim(
                    column_weight, (owner * held.shape[0] + offset) * set_rows, set_rows, 0
                )
                term = jnp.dot(held[offset], weight_set, preferred_element_type=jnp.float32)
                total = total + term.astype(jnp.bfloat16).astype(jnp.float32)
        outputs.append(total)
    summed = jnp.concatenate(outputs, axis=1)
    col_share = model_width // head_count
    own_text = lax.dynamic_slice_in_dim(text, head_index * col_share, col_share, 1)
    dec_out = (own_text.astype(jnp.float32) + summed).astype(jnp.bfloat16)
    return (enc_out, dec_out)


def solution(mesh):
    return jax.shard_map(
        layer_body,
        mesh=mesh,
        in_specs=(
            P("seq", None),
            P(),
            P(),
            P(None, "heads"),
            P("heads"),
            P(None, "heads"),
            P(None, "heads"),
            P("heads"),
            P("heads", None),
            P(),
            P("heads"),
            P(),
            P(),
            P("seq", None),
            P(),
            P("seq", "heads"),
            P("heads"),
            P("heads", "seq"),
            P("seq"),
            P("seq"),
        ),
        out_specs=(P(("seq", "heads"), None), P("seq", "heads")),
        check_vma=False,
    )
```
